128 devices in a mesh: seq: 32 (over z, x, y_lo), tp: 4 (over y_hi, core).
Axes of the slice: x: 4, y: 4 (y_hi: 2, y_lo: 2; y = y_hi * 2 + y_lo), z: 4, core: 2. Of those that a mesh axis runs over, the one named last changes fastest.
Arguments:
- tokens: bfloat16 [16384, 1536], P('seq'), may hold values from -6 to 6
- segment_ids: int32 [16384], P('seq'), may hold values from 0 to 511, never falling along the last dimension, each value on 1 to 4096 neighbouring positions
- attn_gain: float32 [1536], replicated, may hold values from 0.25 to 1.75
- w_query: bfloat16 [1536, 1536], P(None, 'tp'), as said below
- w_kv: bfloat16 [1536, 512], replicated, as said below
- w_out: bfloat16 [1536, 1536], P('tp'), may hold values from -0.15625 to 0.15625
- ffn_gain: float32 [1536], replicated, may hold values from 0.25 to 1.75
- w_gate: bfloat16 [32, 1536, 768], P('seq', None, 'tp'), may hold values from -0.15625 to 0.15625
- w_up: bfloat16 [32, 1536, 768], P('seq', None, 'tp'), may hold values from -0.15625 to 0.15625
- w_down: bfloat16 [32, 768, 1536], P('seq', 'tp'), may hold values from -0.21875 to 0.21875
- expert_picks: int32 [16384, 4], P('seq'), may hold values from 0 to 31, all different within a row; in each aligned block of 512 rows (0 to 511, 512 to 1023, ...) at most 80 rows name the same one
- gate_weights: float32 [16384, 4], P('seq'), may hold values from 0.05 to 1
- page_table: int32 [128], P('seq'), may hold values from 0 to 127, as said below
Outputs:
- layer_out: bfloat16 [16384, 1536], P('seq', 'tp')
- kv_pages: bfloat16 [128, 128, 512], P('seq', None, 'tp')
The draws below stay inside these ranges and needn't reach their ends.
Inputs may be any that keep to these rules, and one draw needn't show every extreme that they name: `segment_ids`: never falls along the pack; each prompt has 1 to 4096 tokens and one has exactly 4096. `expert_picks`: each row names 4 different experts; among the 512 rows of one index of seq no expert is named more than 80 times, a bound that some block reaches. `page_table`: the 4 entries of one index of seq are a permutation of that index's own physical pages, its index times 4 up to 4 more. `w_query`: A projection matrix. `w_kv`: A projection matrix.
All inputs are finite; a program needn't handle non-finite values.
Results may differ from the reference program's by a relative error of at most 0.014.
Values may be sent and summed in bfloat16 or wider, within the bound.
No kernel may reach another device: no remote copies, remote signals or barrier semaphores. Data moves between devices by JAX's collectives and lax.ppermute only.
A program may use at most 128 MiB of HBM per device.

```python
import math
import jax
import jax.numpy as jnp
import numpy as np
from jax import lax

D = 1536
HQ = 12
HK = 2
HD = 128
FF = 768
TOP = 4
TOK_DEV = 512
PAGE = 128
EXPERTS = 32
TOKENS = 16384
LONGEST = 4096
DOCS = 512
CAP = 80
PAGES = 128
PAGES_DEV = 4
N_SEQ = 32


def shared_base(key):
    return jax.random.normal(jax.random.fold_in(key, 11), (D, 2 * HK * HD), jnp.float32)


def draw_w_kv(key, part):
    return (shared_base(key) * D ** (-0.5)).astype(jnp.bfloat16)


def draw_w_query(key, part):
    noise = jax.random.normal(jax.random.fold_in(key, 12), (D, HQ * HD), jnp.float32)
    return (noise * D ** (-0.5)).astype(jnp.bfloat16)


def draw_page_table(key, part):
    blocks = PAGES // PAGES_DEV
    block_keys = jax.random.split(key, blocks)
    orders = jax.vmap(lambda single: jax.random.permutation(single, PAGES_DEV))(block_keys)
    return (orders + jnp.arange(blocks)[:, None] * PAGES_DEV).reshape(PAGES).astype(jnp.int32)


def steps_of(key, shape, cuts, smallest, high):
    level, own = 1.0, jax.random.fold_in(key, 6)
    for axis_at, shards_of in cuts:
        steps = jnp.exp(jax.random.uniform(jax.random.fold_in(own, axis_at), (shards_of,), jnp.float32, smallest / len(cuts), high / len(cuts)))
        level = level * jnp.repeat(steps, shape[axis_at] // shards_of).reshape([-1 if axis == axis_at else 1 for axis in range(len(shape))])
    return level


def profile(amount, total, most, skew):
    portions = [(1 << 20) // math.isqrt(rank ** skew) + 1 for rank in range(2, amount + 1)]
    surplus, given = total - most - (amount - 1), [1] * (amount - 1)
    while surplus > 0:
        free = [i for i in range(amount - 1) if given[i] < most]
        mass, remaining = sum([portions[i] for i in free]), surplus
        for i in free:
            more = min(most - given[i], max(1, remaining * portions[i] // mass), surplus)
            given[i] = given[i] + more
            surplus = surplus - more
    return np.array([most] + given)


def uneven(stream_key, amount, total, limit, slope):
    if amount == 2:
        one = jax.random.randint(stream_key, (), max(1, total - limit), min(limit, total - 1) + 1)
        return jnp.stack([one, total - one])
    tallies = jnp.asarray(profile(amount, total, limit, slope), jnp.int32)
    twos = (amount - 1) // 2
    source_of, sink = tallies[1:1 + 2 * twos:2], tallies[2:2 + 2 * twos:2]
    room = jnp.minimum(source_of - 1, limit - sink)
    passed = jax.random.randint(jax.random.fold_in(stream_key, 1), (twos,), 0, 1 << 20) % (room + 1)
    tallies = tallies.at[1:1 + 2 * twos:2].set(source_of - passed).at[2:2 + 2 * twos:2].set(sink + passed)
    return tallies[jax.random.permutation(jax.random.fold_in(stream_key, 2), amount)]


def deal_out(rng, own, number, rows, number_of, top, limit, lean):
    sequence = jax.random.permutation(rng, number_of)
    packed, usual = shares(number_of, rows * top, limit, lean, True), shares(number_of, rows * top, limit, lean, False)
    places = jnp.arange(number_of)

    def named(lengths, rotation):
        used = int((lengths > 0).sum())
        fixed = max(1, used // 4)
        passed = fixed + (places - fixed + rotation * (used - fixed)) % max(1, number_of - fixed)
        return jnp.zeros((number_of,), jnp.int32).at[sequence[jnp.where(places < fixed, places, passed)]].set(jnp.asarray(lengths, jnp.int32))

    lengths = jnp.where(number % 4 == 0, named(packed, number // 4), named(usual, number - number // 4 - 1))
    mixed = jax.random.permutation(jax.random.fold_in(own, 3), number_of)
    source_of, taker = mixed[0:number_of // 2 * 2:2], mixed[1:number_of // 2 * 2:2]
    slack = jnp.minimum(lengths[source_of] - 1, limit - lengths[taker]) // 2
    slack = jnp.where((source_of == sequence[0]) | (taker == sequence[0]) | (lengths[taker] == 0), 0, jnp.maximum(slack, 0))
    passed = jax.random.randint(jax.random.fold_in(own, 4), (number_of // 2,), 0, 1 << 20) % (slack + 1)
    lengths = lengths.at[source_of].add(-passed).at[taker].add(passed)
    labels = jnp.searchsorted(jnp.cumsum(lengths), jnp.arange(rows * top), side="right").astype(jnp.int32)
    table = labels.reshape(top, rows).T
    table = table[jax.random.permutation(jax.random.fold_in(own, 1), rows)]
    rotation = jax.random.randint(jax.random.fold_in(own, 2), (rows, 1), 0, top)
    return jnp.take_along_axis(table, (jnp.arange(top)[None, :] + rotation) % top, axis=1)


def shares(number_of, total, reach, lean, full):
    weights = [(1 << 20) // math.isqrt(grade ** lean) + 1 for grade in range(1, number_of + 1)]
    largest = reach if full else min(reach, max(-(-total // number_of), total * weights[0] // sum(weights)))
    least = 1 if total - largest >= number_of - 1 else 0
    given, rest = [largest] + [least] * (number_of - 1), total - largest - least * (number_of - 1)
    while rest > 0:
        movable = [i for i in range(1, number_of) if given[i] < largest] or [i for i in range(1, number_of) if given[i] < reach]
        pool, remaining = sum([weights[i] for i in movable]), rest
        for i in movable:
            addition = min(reach - given[i], max(1, remaining * weights[i] // pool), rest)
            given[i] = given[i] + addition
            rest = rest - addition
    return np.array(given)


def normal_values(rng, shape, scale, reach, cuts=(), held_as=jnp.bfloat16):
    level = steps_of(rng, shape, cuts, -0.22, 0.18) if cuts else 1.0
    values = jax.random.normal(rng, shape, jnp.float32) * scale * level
    return jnp.minimum(jnp.maximum(values, -reach), reach).astype(held_as)


def setup_inputs(seed: int = 0) -> dict:
    streams_of = jax.random.split(jax.random.key(seed), 14)
    tokens = normal_values(streams_of[0], (TOKENS, D), 1.0, 6.0, ((0, 32),))
    segment_ids = jnp.searchsorted(jnp.cumsum(uneven(streams_of[1], DOCS, TOKENS, LONGEST, 2)), jnp.arange(TOKENS), side="right").astype(jnp.int32)
    attn_gain = jnp.clip(1.0 + 0.15 * jax.random.normal(streams_of[2], (D,), jnp.float32), 0.25, 1.75)
    w_query = draw_w_query(jax.random.fold_in(streams_of[13], 71), 0)
    w_kv = draw_w_kv(jax.random.fold_in(streams_of[13], 71), 0)
    w_out = normal_values(streams_of[5], (HQ * HD, D), (HQ * HD) ** -0.5, 0.15625, ((0, 4),))
    ffn_gain = jnp.clip(1.0 + 0.15 * jax.random.normal(streams_of[6], (D,), jnp.float32), 0.25, 1.75)
    w_gate = normal_values(streams_of[7], (EXPERTS, D, FF), D ** -0.5, 0.15625, ((0, 32), (2, 4)))
    w_up = normal_values(streams_of[8], (EXPERTS, D, FF), D ** -0.5, 0.15625, ((0, 32), (2, 4)))
    w_down = normal_values(streams_of[9], (EXPERTS, FF, D), FF ** -0.5, 0.21875, ((0, 32), (1, 4)))
    expert_picks_keys = jax.random.split(jax.random.fold_in(streams_of[10], 1), TOKENS // TOK_DEV)
    expert_picks_turns = jax.random.permutation(jax.random.fold_in(streams_of[10], 3), TOKENS // TOK_DEV)
    expert_picks = jax.vmap(lambda own, number: deal_out(jax.random.fold_in(streams_of[10], 2), own, number, TOK_DEV, EXPERTS, TOP, CAP, 2))(expert_picks_keys, expert_picks_turns).reshape((TOKENS, TOP))
    gate_weights = jnp.clip(jnp.exp(math.log(1.0) - 2.9957323 * jax.random.uniform(streams_of[11], (TOKENS, TOP), jnp.float32) ** steps_of(streams_of[11], (TOKENS, TOP), ((0, 32),), -0.2, 0.2)), 0.05, 1.0)
    page_table = draw_page_table(jax.random.fold_in(streams_of[13], 71), 0)
    return dict(tokens=tokens, segment_ids=segment_ids, attn_gain=attn_gain, w_query=w_query, w_kv=w_kv, w_out=w_out, ffn_gain=ffn_gain, w_gate=w_gate, w_up=w_up, w_down=w_down, expert_picks=expert_picks, gate_weights=gate_weights, page_table=page_table)


EPSILON = 1e-06
NEGATIVE = -1e+30

def row_norm(values, gain):
    values = values.astype(jnp.float32)
    factor = lax.rsqrt(lax.optimization_barrier(jnp.mean(values * values, axis=-1, keepdims=True)) + EPSILON)
    return values * factor * gain.astype(jnp.float32)

def attend_block(carry, queries, key_block, value_block, allowed):
    running, total, accum = carry
    scores = jnp.einsum('qhd,kd->qhk', queries.astype(jnp.float32), key_block.astype(jnp.float32)) * HD ** (-0.5)
    open_mask = allowed[:, None, :]
    highest = lax.optimization_barrier(jnp.max(jnp.where(open_mask, scores, NEGATIVE), axis=2))
    renewed = jnp.maximum(running, highest)
    weights = jnp.where(open_mask, jnp.exp(scores - renewed[:, :, None]), 0.0)
    factor = jnp.exp(running - renewed)
    total = total * factor + lax.optimization_barrier(jnp.sum(weights, axis=2))
    rounded = weights.astype(jnp.bfloat16).astype(jnp.float32)
    accum = accum * factor[:, :, None] + jnp.einsum('qhk,kd->qhd', rounded, value_block.astype(jnp.float32))
    return (renewed, total, accum)

def reference(tokens, segment_ids, attn_gain, w_query, w_kv, w_out, ffn_gain, w_gate, w_up, w_down, expert_picks, gate_weights, page_table):
    normed = row_norm(tokens, attn_gain).astype(jnp.bfloat16)
    queries = jnp.dot(normed, w_query, preferred_element_type=jnp.float32).astype(jnp.bfloat16)
    keyval = jnp.dot(normed, w_kv, preferred_element_type=jnp.float32).astype(jnp.bfloat16)
    kv_pages = jnp.zeros((PAGES, PAGE, 2 * HK * HD), jnp.bfloat16).at[page_table].set(keyval.reshape(PAGES, PAGE, 2 * HK * HD))
    group_size = HQ // HK
    query_blocks = queries.reshape(N_SEQ, TOK_DEV, HQ, HD)
    key_all = keyval[:, :HK * HD].reshape(N_SEQ, TOK_DEV, HK, HD)
    value_all = keyval[:, HK * HD:].reshape(N_SEQ, TOK_DEV, HK, HD)
    segment_blocks = segment_ids.reshape(N_SEQ, TOK_DEV)
    numbers = jnp.arange(N_SEQ, dtype=jnp.int32)
    offsets = jnp.arange(TOK_DEV, dtype=jnp.int32)

    def query_block(inputs):
        number, own_queries, own_segments = inputs
        query_index = number * TOK_DEV + offsets

        def key_step(carry, pieces):
            key_number, key_block, value_block, key_segments = pieces
            key_index = key_number * TOK_DEV + offsets
            allowed = (key_segments[None, :] == own_segments[:, None]) & (key_index[None, :] <= query_index[:, None])

            def update(state):
                running, total, accum = state
                parts = []
                for group in range(HK):
                    lower = group * group_size
                    upper = lower + group_size
                    parts.append(attend_block((running[:, lower:upper], total[:, lower:upper], accum[:, lower:upper]), own_queries[:, lower:upper], key_block[:, group], value_block[:, group], allowed))
                return (jnp.concatenate([part[0] for part in parts], axis=1), jnp.concatenate([part[1] for part in parts], axis=1), jnp.concatenate([part[2] for part in parts], axis=1))
            meets = (key_number <= number) & (key_segments[TOK_DEV - 1] >= own_segments[0])
            return (lax.cond(meets, update, lambda state: state, carry), None)
        start_state = (jnp.full((TOK_DEV, HQ), NEGATIVE, jnp.float32), jnp.zeros((TOK_DEV, HQ), jnp.float32), jnp.zeros((TOK_DEV, HQ, HD), jnp.float32))
        final, ignored = lax.scan(key_step, start_state, (numbers, key_all, value_all, segment_blocks))
        return (final[2] / final[1][:, :, None]).astype(jnp.bfloat16).reshape(TOK_DEV, HQ * HD)
    attended = lax.map(query_block, (numbers, query_blocks, segment_blocks)).reshape(TOKENS, HQ * HD)
    residual = tokens.astype(jnp.float32) + jnp.dot(attended, w_out, preferred_element_type=jnp.float32)
    mixed_in = row_norm(residual, ffn_gain).astype(jnp.bfloat16)
    picks = expert_picks.reshape(N_SEQ, TOK_DEV * TOP)
    matches = (picks[:, :, None] == jnp.arange(EXPERTS, dtype=jnp.int32)[None, None, :]).astype(jnp.int32)
    ranks = lax.optimization_barrier(jnp.sum((jnp.cumsum(matches, axis=1) - 1) * matches, axis=2))
    positions = (jnp.arange(N_SEQ, dtype=jnp.int32)[:, None] * CAP + ranks).reshape(-1).astype(jnp.int32)
    flat_picks = expert_picks.reshape(-1).astype(jnp.int32)
    token_index = jnp.arange(TOKENS * TOP, dtype=jnp.int32) // TOP
    table = jnp.full((EXPERTS, N_SEQ * CAP), TOKENS, jnp.int32).at[flat_picks, positions].set(token_index)
    factors = jnp.zeros((EXPERTS, N_SEQ * CAP), jnp.float32).at[flat_picks, positions].set(gate_weights.reshape(-1).astype(jnp.float32))
    padded = jnp.concatenate([mixed_in, jnp.zeros((1, D), jnp.bfloat16)], axis=0)

    def expert_step(summed, inputs):
        gate_matrix, up_matrix, down_matrix, chosen, scales = inputs
        gathered = padded[chosen]
        gate_part = jnp.dot(gathered, gate_matrix, preferred_element_type=jnp.float32)
        up_part = jnp.dot(gathered, up_matrix, preferred_element_type=jnp.float32)
        hidden = (jax.nn.relu(gate_part) * up_part).astype(jnp.bfloat16)
        result = jnp.dot(hidden, down_matrix, preferred_element_type=jnp.float32).astype(jnp.bfloat16)
        return (summed.at[chosen].add(result.astype(jnp.float32) * scales[:, None]), None)
    summed, ignored = lax.scan(expert_step, jnp.zeros((TOKENS + 1, D), jnp.float32), (w_gate, w_up, w_down, table, factors))
    layer_out = (residual + summed[:TOKENS]).astype(jnp.bfloat16)
    return (layer_out, kv_pages)
```

```python
import jax
import jax.numpy as jnp
from jax import lax
from jax.sharding import PartitionSpec as P

HQ = 12
HK = 2
HD = 128


EPSILON = 1e-06
NEGATIVE = -1e30


def shifted(value, axis, steps):
    count = lax.axis_size(axis)
    leading, last = (max(0, -steps), min(count, count - steps))
    return lax.ppermute(value, axis, [(source, source + steps) for source in range(leading, last)])


def row_norm(values, gain):
    values = values.astype(jnp.float32)
    factor = lax.rsqrt(jnp.mean(values * values, axis=-1, keepdims=True) + EPSILON)
    return values * factor * gain


def attend_block(carry, queries, key_block, value_block, allowed):
    running, total, accum = carry
    scores = jnp.einsum(
        "qhd,kd->qhk", queries, key_block, preferred_element_type=jnp.float32
    ) * HD ** (-0.5)
    open_mask = allowed[:, None, :]
    highest = jnp.max(jnp.where(open_mask, scores, NEGATIVE), axis=2)
    renewed = jnp.maximum(running, highest)
    weights = jnp.where(open_mask, jnp.exp(scores - renewed[:, :, None]), 0.0)
    factor = jnp.exp(running - renewed)
    total = total * factor + jnp.sum(weights, axis=2)
    accum = accum * factor[:, :, None] + jnp.einsum(
        "qhk,kd->qhd", weights.astype(jnp.bfloat16), value_block, preferred_element_type=jnp.float32
    )
    return (renewed, total, accum)


def per_device(
    tokens,
    segment_ids,
    attn_gain,
    w_query,
    w_kv,
    w_out,
    ffn_gain,
    w_gate,
    w_up,
    w_down,
    expert_picks,
    gate_weights,
    page_table,
):
    count = tokens.shape[0]
    seq_index = lax.axis_index("seq")
    tp_index = lax.axis_index("tp")
    tp_count = lax.axis_size("tp")
    normed = row_norm(tokens, attn_gain).astype(jnp.bfloat16)
    queries = jnp.dot(normed, w_query, preferred_element_type=jnp.float32).astype(jnp.bfloat16)
    keyval = jnp.dot(normed, w_kv, preferred_element_type=jnp.float32).astype(jnp.bfloat16)
    cache_width = keyval.shape[1] // tp_count
    cache_columns = lax.dynamic_slice_in_dim(keyval, tp_index * cache_width, cache_width, 1)
    page_rows = page_table.shape[0]
    page_length = count // page_rows
    local_pages = page_table - seq_index * page_rows
    kv_pages = (
        jnp.zeros((page_rows, page_length, cache_width), jnp.bfloat16)
        .at[local_pages]
        .set(cache_columns.reshape(page_rows, page_length, cache_width))
    )
    heads = queries.shape[1] // HD
    group = tp_index * heads // (HQ // HK)
    key_head = lax.dynamic_slice_in_dim(keyval, group * HD, HD, 1)
    value_head = lax.dynamic_slice_in_dim(keyval, (HK + group) * HD, HD, 1)
    query_heads = queries.reshape(count, heads, HD)
    query_index = seq_index * count + jnp.arange(count, dtype=jnp.int32)
    all_segments = lax.all_gather(segment_ids, "seq", tiled=True)
    own_piece = jnp.concatenate([key_head, value_head], axis=1)
    reach_steps = lax.axis_size("seq") // 4
    pieces = [own_piece] + [shifted(own_piece, "seq", number) for number in range(1, reach_steps + 1)]

    def visit(carry, piece, number):
        start = (seq_index - number) * count
        key_index = start + jnp.arange(count, dtype=jnp.int32)
        segment_piece = lax.dynamic_slice_in_dim(all_segments, jnp.maximum(start, 0), count)
        allowed = (
            (segment_piece[None, :] == segment_ids[:, None])
            & (key_index[None, :] <= query_index[:, None])
            & (key_index[None, :] >= 0)
        )
        return attend_block(carry, query_heads, piece[:, :HD], piece[:, HD:], allowed)

    state = (
        jnp.full((count, heads), NEGATIVE, jnp.float32),
        jnp.zeros((count, heads), jnp.float32),
        jnp.zeros((count, heads, HD), jnp.float32),
    )
    for number, piece in enumerate(pieces):
        state = visit(state, piece, number)
    attended = (state[2] / state[1][:, :, None]).astype(jnp.bfloat16).reshape(count, heads * HD)
    projected = jnp.dot(attended, w_out, preferred_element_type=jnp.float32)
    experts = lax.axis_size("seq") * w_gate.shape[0]
    choose = expert_picks.shape[1]
    capacity = count * choose * 5 // (4 * experts)
    share = capacity // tp_count
    slots = experts * share
    onehot = (expert_picks[:, :, None] == jnp.arange(experts, dtype=jnp.int32)[None, None, :]).astype(
        jnp.float32
    )
    earlier = (
        jnp.arange(count, dtype=jnp.int32)[:, None] > jnp.arange(count, dtype=jnp.int32)[None, :]
    ).astype(jnp.bfloat16)
    before = jnp.dot(
        earlier, jnp.sum(onehot, axis=1).astype(jnp.bfloat16), preferred_element_type=jnp.float32
    )
    ranks = jnp.sum(before[:, None, :] * onehot, axis=2).astype(jnp.int32)
    owner = ranks // share
    slot = expert_picks * share + ranks % share
    token_of = jnp.broadcast_to(jnp.arange(count, dtype=jnp.int32)[:, None], expert_picks.shape)
    table = (
        jnp.full((slots,), count, jnp.int32)
        .at[jnp.where(owner == tp_index, slot, slots).reshape(-1)]
        .set(token_of.reshape(-1), mode="drop")
    )
    part_width = tokens.shape[1] // tp_count
    summed = lax.psum(projected.astype(jnp.bfloat16), "tp").astype(jnp.float32)
    residual = tokens.astype(jnp.float32) + summed
    mixed_in = row_norm(residual, ffn_gain).astype(jnp.bfloat16)
    columns = mixed_in.shape[1]
    padded = jnp.concatenate([mixed_in, jnp.zeros((1, columns), jnp.bfloat16)], axis=0)
    arrived = lax.all_to_all(padded[table], "seq", split_axis=0, concat_axis=0, tiled=True)
    gate_full = lax.all_gather(w_gate[0], "tp", axis=1, tiled=True)
    up_full = lax.all_gather(w_up[0], "tp", axis=1, tiled=True)
    down_full = lax.all_gather(w_down[0], "tp", axis=0, tiled=True)
    gate_part = jnp.dot(arrived, gate_full, preferred_element_type=jnp.float32)
    up_part = jnp.dot(arrived, up_full, preferred_element_type=jnp.float32)
    hidden = (jax.nn.relu(gate_part) * up_part).astype(jnp.bfloat16)
    expert_out = jnp.dot(hidden, down_full, preferred_element_type=jnp.float32).astype(jnp.bfloat16)
    returned = lax.all_to_all(expert_out, "seq", split_axis=0, concat_axis=0, tiled=True)
    mine = lax.all_to_all(returned, "tp", split_axis=1, concat_axis=0, tiled=True)
    residual_part = lax.dynamic_slice_in_dim(residual, tp_index * part_width, part_width, 1)
    gathered = mine[jnp.minimum(owner * slots + slot, tp_count * slots - 1)].astype(jnp.float32)
    mixture = jnp.sum(gathered * gate_weights[:, :, None], axis=1)
    layer_out = (residual_part + mixture).astype(jnp.bfloat16)
    return (layer_out, kv_pages)


def solution(mesh):
    placed = (
        P("seq", None),
        P("seq"),
        P(),
        P(None, "tp"),
        P(),
        P("tp", None),
        P(),
        P("seq", None, "tp"),
        P("seq", None, "tp"),
        P("seq", "tp", None),
        P("seq", None),
        P("seq", None),
        P("seq"),
    )
    return jax.shard_map(
        per_device,
        mesh=mesh,
        in_specs=placed,
        out_specs=(P("seq", "tp"), P("seq", None, "tp")),
        check_vma=False,
    )
```

```python
import jax
import jax.numpy as jnp
from jax import lax
from jax.sharding import PartitionSpec as P

HQ = 12
HK = 2
HD = 128


EPSILON = 1e-06
NEGATIVE = -1e30


def shifted(value, axis, steps):
    count = lax.axis_size(axis)
    leading, last = (max(0, -steps), min(count, count - steps))
    return lax.ppermute(value, axis, [(source, source + steps) for source in range(leading, last)])


def row_norm(values, gain):
    values = values.astype(jnp.float32)
    factor = lax.rsqrt(jnp.mean(values * values, axis=-1, keepdims=True) + EPSILON)
    return values * factor * gain


def attend_block(carry, queries, key_block, value_block, allowed):
    running, total, accum = carry
    scores = jnp.einsum(
        "qhd,kd->qhk", queries, key_block, preferred_element_type=jnp.float32
    ) * HD ** (-0.5)
    open_mask = allowed[:, None, :]
    highest = jnp.max(jnp.where(open_mask, scores, NEGATIVE), axis=2)
    renewed = jnp.maximum(running, highest)
    weights = jnp.where(open_mask, jnp.exp(scores - renewed[:, :, None]), 0.0)
    factor = jnp.exp(running - renewed)
    total = total * factor + jnp.sum(weights, axis=2)
    accum = accum * factor[:, :, None] + jnp.einsum(
        "qhk,kd->qhd", weights.astype(jnp.bfloat16), value_block, preferred_element_type=jnp.float32
    )
    return (renewed, total, accum)


def per_device(
    tokens,
    segment_ids,
    attn_gain,
    w_query,
    w_kv,
    w_out,
    ffn_gain,
    w_gate,
    w_up,
    w_down,
    expert_picks,
    gate_weights,
    page_table,
):
    count = tokens.shape[0]
    seq_index = lax.axis_index("seq")
    tp_index = lax.axis_index("tp")
    tp_count = lax.axis_size("tp")
    normed = row_norm(tokens, attn_gain).astype(jnp.bfloat16)
    queries = jnp.dot(normed, w_query, preferred_element_type=jnp.float32).astype(jnp.bfloat16)
    keyval = jnp.dot(normed, w_kv, preferred_element_type=jnp.float32).astype(jnp.bfloat16)
    cache_width = keyval.shape[1] // tp_count
    cache_columns = lax.dynamic_slice_in_dim(keyval, tp_index * cache_width, cache_width, 1)
    page_rows = page_table.shape[0]
    page_length = count // page_rows
    local_pages = page_table - seq_index * page_rows
    kv_pages = (
        jnp.zeros((page_rows, page_length, cache_width), jnp.bfloat16)
        .at[local_pages]
        .set(cache_columns.reshape(page_rows, page_length, cache_width))
    )
    heads = queries.shape[1] // HD
    group = tp_index * heads // (HQ // HK)
    key_head = lax.dynamic_slice_in_dim(keyval, group * HD, HD, 1)
    value_head = lax.dynamic_slice_in_dim(keyval, (HK + group) * HD, HD, 1)
    query_heads = queries.reshape(count, heads, HD)
    query_index = seq_index * count + jnp.arange(count, dtype=jnp.int32)
    width = 2 * HD
    code_rows = 2 * count // width
    code = jnp.stack([segment_ids // 256, segment_ids % 256]).astype(jnp.bfloat16).reshape(code_rows, width)
    code = jnp.concatenate([code, jnp.zeros((16 - code_rows % 16, width), jnp.bfloat16)], axis=0)
    own_piece = jnp.concatenate([jnp.concatenate([key_head, value_head], axis=1), code], axis=0)
    reach_steps = lax.axis_size("seq") // 4
    pieces = [own_piece] + [shifted(own_piece, "seq", number) for number in range(1, reach_steps + 1)]

    def visit(carry, piece, number):
        start = (seq_index - number) * count
        key_index = start + jnp.arange(count, dtype=jnp.int32)
        coded = piece[count : count + code_rows].reshape(2, count).astype(jnp.int32)
        segment_piece = coded[0] * 256 + coded[1]
        allowed = (
            (segment_piece[None, :] == segment_ids[:, None])
            & (key_index[None, :] <= query_index[:, None])
            & (key_index[None, :] >= 0)
        )
        return attend_block(carry, query_heads, piece[:count, :HD], piece[:count, HD:], allowed)

    state = (
        jnp.full((count, heads), NEGATIVE, jnp.float32),
        jnp.zeros((count, heads), jnp.float32),
        jnp.zeros((count, heads, HD), jnp.float32),
    )
    for number, piece in enumerate(pieces):
        state = visit(state, piece, number)
    attended = (state[2] / state[1][:, :, None]).astype(jnp.bfloat16).reshape(count, heads * HD)
    hidden_part = w_gate.shape[2]
    packed = jnp.concatenate([w_gate[0], w_up[0], w_down[0].T], axis=1)
    weight_parts = [packed] + [
        lax.ppermute(packed, "tp", [(source, (source + number) % tp_count) for source in range(tp_count)])
        for number in range(1, tp_count)
    ]
    attended, weight_parts = lax.optimization_barrier((attended, weight_parts))
    projected = jnp.dot(attended, w_out, preferred_element_type=jnp.float32)
    experts = lax.axis_size("seq") * w_gate.shape[0]
    choose = expert_picks.shape[1]
    capacity = count * choose * 5 // (4 * experts)
    share = capacity // tp_count
    slots = experts * share
    onehot = (expert_picks[:, :, None] == jnp.arange(experts, dtype=jnp.int32)[None, None, :]).astype(
        jnp.float32
    )
    earlier = (
        jnp.arange(count, dtype=jnp.int32)[:, None] > jnp.arange(count, dtype=jnp.int32)[None, :]
    ).astype(jnp.bfloat16)
    before = jnp.dot(
        earlier, jnp.sum(onehot, axis=1).astype(jnp.bfloat16), preferred_element_type=jnp.float32
    )
    ranks = jnp.sum(before[:, None, :] * onehot, axis=2).astype(jnp.int32)
    owner = ranks // share
    slot = expert_picks * share + ranks % share
    token_of = jnp.broadcast_to(jnp.arange(count, dtype=jnp.int32)[:, None], expert_picks.shape)
    table = (
        jnp.full((slots,), count, jnp.int32)
        .at[jnp.where(owner == tp_index, slot, slots).reshape(-1)]
        .set(token_of.reshape(-1), mode="drop")
    )
    part_width = tokens.shape[1] // tp_count
    summed = lax.psum(projected.astype(jnp.bfloat16), "tp").astype(jnp.float32)
    residual = tokens.astype(jnp.float32) + summed
    mixed_in = row_norm(residual, ffn_gain).astype(jnp.bfloat16)
    columns = mixed_in.shape[1]
    padded = jnp.concatenate([mixed_in, jnp.zeros((1, columns), jnp.bfloat16)], axis=0)
    arrived = lax.all_to_all(padded[table], "seq", split_axis=0, concat_axis=0, tiled=True)
    gate_full = jnp.concatenate([part[:, :hidden_part] for part in weight_parts], axis=1)
    up_full = jnp.concatenate([part[:, hidden_part : 2 * hidden_part] for part in weight_parts], axis=1)
    down_full = jnp.concatenate([part[:, 2 * hidden_part :] for part in weight_parts], axis=1).T
    gate_part = jnp.dot(arrived, gate_full, preferred_element_type=jnp.float32)
    up_part = jnp.dot(arrived, up_full, preferred_element_type=jnp.float32)
    hidden = (jax.nn.relu(gate_part) * up_part).astype(jnp.bfloat16)
    expert_out = jnp.dot(hidden, down_full, preferred_element_type=jnp.float32).astype(jnp.bfloat16)
    returned = lax.all_to_all(expert_out, "seq", split_axis=0, concat_axis=0, tiled=True)
    mine = lax.all_to_all(returned, "tp", split_axis=1, concat_axis=0, tiled=True)
    residual_part = lax.dynamic_slice_in_dim(residual, tp_index * part_width, part_width, 1)
    gathered = mine[jnp.minimum(owner * slots + slot, tp_count * slots - 1)].astype(jnp.float32)
    mixture = jnp.sum(gathered * gate_weights[:, :, None], axis=1)
    layer_out = (residual_part + mixture).astype(jnp.bfloat16)
    return (layer_out, kv_pages)


def solution(mesh):
    placed = (
        P("seq", None),
        P("seq"),
        P(),
        P(None, "tp"),
        P(),
        P("tp", None),
        P(),
        P("seq", None, "tp"),
        P("seq", None, "tp"),
        P("seq", "tp", None),
        P("seq", None),
        P("seq", None),
        P("seq"),
    )
    return jax.shard_map(
        per_device,
        mesh=mesh,
        in_specs=placed,
        out_specs=(P("seq", "tp"), P("seq", None, "tp")),
        check_vma=False,
    )
```

```python
import jax
import jax.numpy as jnp
from jax import lax
from jax.sharding import PartitionSpec as P

HQ = 12
HK = 2
HD = 128


EPSILON = 1e-06
NEGATIVE = -1e30


def shifted(value, axis, steps):
    count = lax.axis_size(axis)
    leading, last = (max(0, -steps), min(count, count - steps))
    return lax.ppermute(value, axis, [(source, source + steps) for source in range(leading, last)])


def row_norm(values, gain):
    values = values.astype(jnp.float32)
    factor = lax.rsqrt(jnp.mean(values * values, axis=-1, keepdims=True) + EPSILON)
    return values * factor * gain


def attend_block(carry, queries, key_block, value_block, allowed):
    running, total, accum = carry
    scores = jnp.einsum(
        "qhd,kd->qhk", queries, key_block, preferred_element_type=jnp.float32
    ) * HD ** (-0.5)
    open_mask = allowed[:, None, :]
    highest = jnp.max(jnp.where(open_mask, scores, NEGATIVE), axis=2)
    renewed = jnp.maximum(running, highest)
    weights = jnp.where(open_mask, jnp.exp(scores - renewed[:, :, None]), 0.0)
    factor = jnp.exp(running - renewed)
    total = total * factor + jnp.sum(weights, axis=2)
    accum = accum * factor[:, :, None] + jnp.einsum(
        "qhk,kd->qhd", weights.astype(jnp.bfloat16), value_block, preferred_element_type=jnp.float32
    )
    return (renewed, total, accum)


def per_device(
    tokens,
    segment_ids,
    attn_gain,
    w_query,
    w_kv,
    w_out,
    ffn_gain,
    w_gate,
    w_up,
    w_down,
    expert_picks,
    gate_weights,
    page_table,
):
    count = tokens.shape[0]
    seq_index = lax.axis_index("seq")
    tp_index = lax.axis_index("tp")
    tp_count = lax.axis_size("tp")
    normed = row_norm(tokens, attn_gain).astype(jnp.bfloat16)
    queries = jnp.dot(normed, w_query, preferred_element_type=jnp.float32).astype(jnp.bfloat16)
    keyval = jnp.dot(normed, w_kv, preferred_element_type=jnp.float32).astype(jnp.bfloat16)
    cache_width = keyval.shape[1] // tp_count
    cache_columns = lax.dynamic_slice_in_dim(keyval, tp_index * cache_width, cache_width, 1)
    page_rows = page_table.shape[0]
    page_length = count // page_rows
    local_pages = page_table - seq_index * page_rows
    kv_pages = (
        jnp.zeros((page_rows, page_length, cache_width), jnp.bfloat16)
        .at[local_pages]
        .set(cache_columns.reshape(page_rows, page_length, cache_width))
    )
    heads = queries.shape[1] // HD
    group = tp_index * heads // (HQ // HK)
    key_head = lax.dynamic_slice_in_dim(keyval, group * HD, HD, 1)
    value_head = lax.dynamic_slice_in_dim(keyval, (HK + group) * HD, HD, 1)
    query_heads = queries.reshape(count, heads, HD)
    query_index = seq_index * count + jnp.arange(count, dtype=jnp.int32)
    width = 2 * HD
    code_rows = 2 * count // width
    code = jnp.stack([segment_ids // 256, segment_ids % 256]).astype(jnp.bfloat16).reshape(code_rows, width)
    code = jnp.concatenate([code, jnp.zeros((16 - code_rows % 16, width), jnp.bfloat16)], axis=0)
    own_piece = jnp.concatenate([jnp.concatenate([key_head, value_head], axis=1), code], axis=0)
    reach_steps = lax.axis_size("seq") // 4
    pieces = [own_piece] + [shifted(own_piece, "seq", number) for number in range(1, reach_steps + 1)]

    def visit(carry, piece, number):
        start = (seq_index - number) * count
        key_index = start + jnp.arange(count, dtype=jnp.int32)
        coded = piece[count : count + code_rows].reshape(2, count).astype(jnp.int32)
        segment_piece = coded[0] * 256 + coded[1]
        allowed = (
            (segment_piece[None, :] == segment_ids[:, None])
            & (key_index[None, :] <= query_index[:, None])
            & (key_index[None, :] >= 0)
        )
        return attend_block(carry, query_heads, piece[:count, :HD], piece[:count, HD:], allowed)

    state = (
        jnp.full((count, heads), NEGATIVE, jnp.float32),
        jnp.zeros((count, heads), jnp.float32),
        jnp.zeros((count, heads, HD), jnp.float32),
    )
    for number, piece in enumerate(pieces):
        state = visit(state, piece, number)
    attended = (state[2] / state[1][:, :, None]).astype(jnp.bfloat16).reshape(count, heads * HD)
    hidden_part = w_gate.shape[2]
    packed = jnp.concatenate([w_gate[0], w_up[0], w_down[0].T], axis=1)
    weight_parts = [packed] + [
        lax.ppermute(packed, "tp", [(source, (source + number) % tp_count) for source in range(tp_count)])
        for number in range(1, tp_count)
    ]
    projected = jnp.dot(attended, w_out, preferred_element_type=jnp.float32)
    experts = lax.axis_size("seq") * w_gate.shape[0]
    choose = expert_picks.shape[1]
    capacity = count * choose * 5 // (4 * experts)
    share = capacity // tp_count
    slots = experts * share
    onehot = (expert_picks[:, :, None] == jnp.arange(experts, dtype=jnp.int32)[None, None, :]).astype(
        jnp.float32
    )
    earlier = (
        jnp.arange(count, dtype=jnp.int32)[:, None] > jnp.arange(count, dtype=jnp.int32)[None, :]
    ).astype(jnp.bfloat16)
    before = jnp.dot(
        earlier, jnp.sum(onehot, axis=1).astype(jnp.bfloat16), preferred_element_type=jnp.float32
    )
    ranks = jnp.sum(before[:, None, :] * onehot, axis=2).astype(jnp.int32)
    owner = ranks // share
    slot = expert_picks * share + ranks % share
    mine_slot = jnp.where(owner == tp_index, slot, slots)
    slot_range = jnp.arange(slots, dtype=jnp.int32)
    placing = jnp.sum(
        (mine_slot[:, :, None] == slot_range[None, None, :]).astype(jnp.bfloat16), axis=1
    ).T
    part_width = tokens.shape[1] // tp_count
    summed = lax.psum(projected.astype(jnp.bfloat16), "tp")
    summed, weight_parts = lax.optimization_barrier((summed, weight_parts))
    summed = summed.astype(jnp.float32)
    residual = tokens.astype(jnp.float32) + summed
    mixed_in = row_norm(residual, ffn_gain).astype(jnp.bfloat16)
    columns = mixed_in.shape[1]
    rows = jnp.dot(placing, mixed_in, preferred_element_type=jnp.float32).astype(jnp.bfloat16)
    arrived = lax.all_to_all(rows, "seq", split_axis=0, concat_axis=0, tiled=True)
    gate_full = jnp.concatenate([part[:, :hidden_part] for part in weight_parts], axis=1)
    up_full = jnp.concatenate([part[:, hidden_part : 2 * hidden_part] for part in weight_parts], axis=1)
    down_full = jnp.concatenate([part[:, 2 * hidden_part :] for part in weight_parts], axis=1).T
    gate_part = jnp.dot(arrived, gate_full, preferred_element_type=jnp.float32)
    up_part = jnp.dot(arrived, up_full, preferred_element_type=jnp.float32)
    hidden = (jax.nn.relu(gate_part) * up_part).astype(jnp.bfloat16)
    expert_out = jnp.dot(hidden, down_full, preferred_element_type=jnp.float32).astype(jnp.bfloat16)
    returned = lax.all_to_all(expert_out, "seq", split_axis=0, concat_axis=0, tiled=True)
    mine = lax.all_to_all(returned, "tp", split_axis=1, concat_axis=0, tiled=True)
    residual_part = lax.dynamic_slice_in_dim(residual, tp_index * part_width, part_width, 1)
    every_slot = jnp.arange(tp_count * slots, dtype=jnp.int32)
    picked = (owner * slots + slot)[:, :, None] == every_slot[None, None, :]
    scales = jnp.sum(jnp.where(picked, gate_weights[:, :, None], 0.0), axis=1)
    high = scales.astype(jnp.bfloat16)
    low = (scales - high.astype(jnp.float32)).astype(jnp.bfloat16)
    mixture = jnp.dot(high, mine, preferred_element_type=jnp.float32) + jnp.dot(
        low, mine, preferred_element_type=jnp.float32
    )
    layer_out = (residual_part + mixture).astype(jnp.bfloat16)
    return (layer_out, kv_pages)


def solution(mesh):
    placed = (
        P("seq", None),
        P("seq"),
        P(),
        P(None, "tp"),
        P(),
        P("tp", None),
        P(),
        P("seq", None, "tp"),
        P("seq", None, "tp"),
        P("seq", "tp", None),
        P("seq", None),
        P("seq", None),
        P("seq"),
    )
    return jax.shard_map(
        per_device,
        mesh=mesh,
        in_specs=placed,
        out_specs=(P("seq", "tp"), P("seq", None, "tp")),
        check_vma=False,
    )
```

```python
import jax
import jax.numpy as jnp
from jax import lax
from jax.sharding import PartitionSpec as P

HQ = 12
HK = 2
HD = 128


EPSILON = 1e-06
NEGATIVE = -1e30


def shifted(value, axis, steps):
    count = lax.axis_size(axis)
    leading, last = (max(0, -steps), min(count, count - steps))
    return lax.ppermute(value, axis, [(source, source + steps) for source in range(leading, last)])


def row_norm(values, gain):
    values = values.astype(jnp.float32)
    factor = lax.rsqrt(jnp.mean(values * values, axis=-1, keepdims=True) + EPSILON)
    return values * factor * gain


def attend_block(carry, queries, key_block, value_block, allowed):
    running, total, accum = carry
    scores = jnp.einsum(
        "qhd,kd->qhk", queries, key_block, preferred_element_type=jnp.float32
    ) * HD ** (-0.5)
    open_mask = allowed[:, None, :]
    highest = jnp.max(jnp.where(open_mask, scores, NEGATIVE), axis=2)
    renewed = jnp.maximum(running, highest)
    weights = jnp.where(open_mask, jnp.exp(scores - renewed[:, :, None]), 0.0)
    factor = jnp.exp(running - renewed)
    total = total * factor + jnp.sum(weights, axis=2)
    accum = accum * factor[:, :, None] + jnp.einsum(
        "qhk,kd->qhd", weights.astype(jnp.bfloat16), value_block, preferred_element_type=jnp.float32
    )
    return (renewed, total, accum)


def per_device(
    tokens,
    segment_ids,
    attn_gain,
    w_query,
    w_kv,
    w_out,
    ffn_gain,
    w_gate,
    w_up,
    w_down,
    expert_picks,
    gate_weights,
    page_table,
):
    count = tokens.shape[0]
    seq_index = lax.axis_index("seq")
    tp_index = lax.axis_index("tp")
    tp_count = lax.axis_size("tp")
    normed = row_norm(tokens, attn_gain).astype(jnp.bfloat16)
    queries = jnp.dot(normed, w_query, preferred_element_type=jnp.float32).astype(jnp.bfloat16)
    keyval = jnp.dot(normed, w_kv, preferred_element_type=jnp.float32).astype(jnp.bfloat16)
    cache_width = keyval.shape[1] // tp_count
    cache_columns = lax.dynamic_slice_in_dim(keyval, tp_index * cache_width, cache_width, 1)
    page_rows = page_table.shape[0]
    page_length = count // page_rows
    local_pages = page_table - seq_index * page_rows
    kv_pages = (
        jnp.zeros((page_rows, page_length, cache_width), jnp.bfloat16)
        .at[local_pages]
        .set(cache_columns.reshape(page_rows, page_length, cache_width))
    )
    heads = queries.shape[1] // HD
    group = tp_index * heads // (HQ // HK)
    key_head = lax.dynamic_slice_in_dim(keyval, group * HD, HD, 1)
    value_head = lax.dynamic_slice_in_dim(keyval, (HK + group) * HD, HD, 1)
    query_heads = queries.reshape(count, heads, HD)
    query_index = seq_index * count + jnp.arange(count, dtype=jnp.int32)
    width = 2 * HD
    code_rows = 2 * count // width
    code = jnp.stack([segment_ids // 256, segment_ids % 256]).astype(jnp.bfloat16).reshape(code_rows, width)
    code = jnp.concatenate([code, jnp.zeros((16 - code_rows % 16, width), jnp.bfloat16)], axis=0)
    own_piece = jnp.concatenate([jnp.concatenate([key_head, value_head], axis=1), code], axis=0)
    reach_steps = lax.axis_size("seq") // 4
    pieces = [own_piece] + [shifted(own_piece, "seq", number) for number in range(1, reach_steps + 1)]

    def visit(carry, piece, number):
        start = (seq_index - number) * count
        key_index = start + jnp.arange(count, dtype=jnp.int32)
        coded = piece[count : count + code_rows].reshape(2, count).astype(jnp.int32)
        segment_piece = coded[0] * 256 + coded[1]
        allowed = (
            (segment_piece[None, :] == segment_ids[:, None])
            & (key_index[None, :] <= query_index[:, None])
            & (key_index[None, :] >= 0)
        )
        return attend_block(carry, query_heads, piece[:count, :HD], piece[:count, HD:], allowed)

    state = (
        jnp.full((count, heads), NEGATIVE, jnp.float32),
        jnp.zeros((count, heads), jnp.float32),
        jnp.zeros((count, heads, HD), jnp.float32),
    )
    for number, piece in enumerate(pieces):
        state = visit(state, piece, number)
    attended = (state[2] / state[1][:, :, None]).astype(jnp.bfloat16).reshape(count, heads * HD)
    hidden_part = w_gate.shape[2]
    packed = jnp.concatenate([w_gate[0], w_up[0], w_down[0].T], axis=1)
    weight_parts = [packed] + [
        lax.ppermute(packed, "tp", [(source, (source + number) % tp_count) for source in range(tp_count)])
        for number in range(1, tp_count)
    ]
    projected = jnp.dot(attended, w_out, preferred_element_type=jnp.float32)
    experts = lax.axis_size("seq") * w_gate.shape[0]
    choose = expert_picks.shape[1]
    capacity = count * choose * 5 // (4 * experts)
    share = capacity // tp_count
    slots = experts * share
    onehot = (expert_picks[:, :, None] == jnp.arange(experts, dtype=jnp.int32)[None, None, :]).astype(
        jnp.float32
    )
    earlier = (
        jnp.arange(count, dtype=jnp.int32)[:, None] > jnp.arange(count, dtype=jnp.int32)[None, :]
    ).astype(jnp.bfloat16)
    before = jnp.dot(
        earlier, jnp.sum(onehot, axis=1).astype(jnp.bfloat16), preferred_element_type=jnp.float32
    )
    ranks = jnp.sum(before[:, None, :] * onehot, axis=2).astype(jnp.int32)
    owner = ranks // share
    slot = expert_picks * share + ranks % share
    mine_slot = jnp.where(owner == tp_index, slot, slots)
    slot_range = jnp.arange(slots, dtype=jnp.int32)
    placing = jnp.sum(
        (mine_slot[:, :, None] == slot_range[None, None, :]).astype(jnp.bfloat16), axis=1
    ).T
    part_width = tokens.shape[1] // tp_count
    summed = lax.psum(projected.astype(jnp.bfloat16), "tp")
    summed, weight_parts = lax.optimization_barrier((summed, weight_parts))
    summed = summed.astype(jnp.float32)
    residual = tokens.astype(jnp.float32) + summed
    mixed_in = row_norm(residual, ffn_gain).astype(jnp.bfloat16)
    columns = mixed_in.shape[1]
    rows = jnp.dot(placing, mixed_in, preferred_element_type=jnp.float32).astype(jnp.bfloat16)
    arrived = lax.all_to_all(rows, "seq", split_axis=0, concat_axis=0, tiled=True)
    gate_full = jnp.concatenate([part[:, :hidden_part] for part in weight_parts], axis=1)
    up_full = jnp.concatenate([part[:, hidden_part : 2 * hidden_part] for part in weight_parts], axis=1)
    down_full = jnp.concatenate([part[:, 2 * hidden_part :] for part in weight_parts], axis=1).T
    gate_part = jnp.dot(arrived, gate_full, preferred_element_type=jnp.float32)
    up_part = jnp.dot(arrived, up_full, preferred_element_type=jnp.float32)
    hidden = (jax.nn.relu(gate_part) * up_part).astype(jnp.bfloat16)
    expert_out = jnp.dot(hidden, down_full, preferred_element_type=jnp.float32).astype(jnp.bfloat16)
    sources = lax.axis_size("seq")
    outgoing = (
        expert_out.reshape(sources, share, tp_count, part_width)
        .transpose(0, 2, 1, 3)
        .reshape(sources * tp_count * share, part_width)
    )
    mine = lax.all_to_all(outgoing, ("seq", "tp"), split_axis=0, concat_axis=0, tiled=True)
    residual_part = lax.dynamic_slice_in_dim(residual, tp_index * part_width, part_width, 1)
    every_slot = jnp.arange(experts * capacity, dtype=jnp.int32)
    picked = (expert_picks * capacity + ranks)[:, :, None] == every_slot[None, None, :]
    scales = jnp.sum(jnp.where(picked, gate_weights[:, :, None], 0.0), axis=1)
    high = scales.astype(jnp.bfloat16)
    low = (scales - high.astype(jnp.float32)).astype(jnp.bfloat16)
    mixture = jnp.dot(high, mine, preferred_element_type=jnp.float32) + jnp.dot(
        low, mine, preferred_element_type=jnp.float32
    )
    layer_out = (residual_part + mixture).astype(jnp.bfloat16)
    return (layer_out, kv_pages)


def solution(mesh):
    placed = (
        P("seq", None),
        P("seq"),
        P(),
        P(None, "tp"),
        P(),
        P("tp", None),
        P(),
        P("seq", None, "tp"),
        P("seq", None, "tp"),
        P("seq", "tp", None),
        P("seq", None),
        P("seq", None),
        P("seq"),
    )
    return jax.shard_map(
        per_device,
        mesh=mesh,
        in_specs=placed,
        out_specs=(P("seq", "tp"), P("seq", None, "tp")),
        check_vma=False,
    )
```

```python
import jax
import jax.numpy as jnp
from jax import lax
from jax.sharding import PartitionSpec as P

HQ = 12
HK = 2
HD = 128


EPSILON = 1e-06
NEGATIVE = -1e30


def shifted(value, axis, steps):
    count = lax.axis_size(axis)
    leading, last = (max(0, -steps), min(count, count - steps))
    return lax.ppermute(value, axis, [(source, source + steps) for source in range(leading, last)])


def row_norm(values, gain):
    values = values.astype(jnp.float32)
    factor = lax.rsqrt(jnp.mean(values * values, axis=-1, keepdims=True) + EPSILON)
    return values * factor * gain


def attend_block(carry, queries, key_block, value_block, allowed):
    running, total, accum = carry
    scores = jnp.einsum(
        "qhd,kd->qhk", queries, key_block, preferred_element_type=jnp.float32
    ) * HD ** (-0.5)
    open_mask = allowed[:, None, :]
    highest = jnp.max(jnp.where(open_mask, scores, NEGATIVE), axis=2)
    renewed = jnp.maximum(running, highest)
    weights = jnp.where(open_mask, jnp.exp(scores - renewed[:, :, None]), 0.0)
    factor = jnp.exp(running - renewed)
    total = total * factor + jnp.sum(weights, axis=2)
    accum = accum * factor[:, :, None] + jnp.einsum(
        "qhk,kd->qhd", weights.astype(jnp.bfloat16), value_block, preferred_element_type=jnp.float32
    )
    return (renewed, total, accum)


def per_device(
    tokens,
    segment_ids,
    attn_gain,
    w_query,
    w_kv,
    w_out,
    ffn_gain,
    w_gate,
    w_up,
    w_down,
    expert_picks,
    gate_weights,
    page_table,
):
    count = tokens.shape[0]
    seq_index = lax.axis_index("seq")
    tp_index = lax.axis_index("tp")
    tp_count = lax.axis_size("tp")
    normed = row_norm(tokens, attn_gain).astype(jnp.bfloat16)
    queries = jnp.dot(normed, w_query, preferred_element_type=jnp.float32).astype(jnp.bfloat16)
    keyval = jnp.dot(normed, w_kv, preferred_element_type=jnp.float32).astype(jnp.bfloat16)
    cache_width = keyval.shape[1] // tp_count
    cache_columns = lax.dynamic_slice_in_dim(keyval, tp_index * cache_width, cache_width, 1)
    page_rows = page_table.shape[0]
    page_length = count // page_rows
    local_pages = page_table - seq_index * page_rows
    kv_pages = (
        jnp.zeros((page_rows, page_length, cache_width), jnp.bfloat16)
        .at[local_pages]
        .set(cache_columns.reshape(page_rows, page_length, cache_width))
    )
    heads = queries.shape[1] // HD
    group = tp_index * heads // (HQ // HK)
    key_head = lax.dynamic_slice_in_dim(keyval, group * HD, HD, 1)
    value_head = lax.dynamic_slice_in_dim(keyval, (HK + group) * HD, HD, 1)
    query_heads = queries.reshape(count, heads, HD)
    query_index = seq_index * count + jnp.arange(count, dtype=jnp.int32)
    width = 2 * HD
    code_rows = 2 * count // width
    code = jnp.stack([segment_ids // 256, segment_ids % 256]).astype(jnp.bfloat16).reshape(code_rows, width)
    code = jnp.concatenate([code, jnp.zeros((16 - code_rows % 16, width), jnp.bfloat16)], axis=0)
    own_piece = jnp.concatenate([jnp.concatenate([key_head, value_head], axis=1), code], axis=0)
    reach_steps = lax.axis_size("seq") // 4
    pieces = [own_piece] + [shifted(own_piece, "seq", number) for number in range(1, reach_steps + 1)]

    def visit(carry, piece, number):
        start = (seq_index - number) * count
        key_index = start + jnp.arange(count, dtype=jnp.int32)
        coded = piece[count : count + code_rows].reshape(2, count).astype(jnp.int32)
        segment_piece = coded[0] * 256 + coded[1]
        allowed = (
            (segment_piece[None, :] == segment_ids[:, None])
            & (key_index[None, :] <= query_index[:, None])
            & (key_index[None, :] >= 0)
        )
        return attend_block(carry, query_heads, piece[:count, :HD], piece[:count, HD:], allowed)

    state = (
        jnp.full((count, heads), NEGATIVE, jnp.float32),
        jnp.zeros((count, heads), jnp.float32),
        jnp.zeros((count, heads, HD), jnp.float32),
    )
    for number, piece in enumerate(pieces):
        state = visit(state, piece, number)
    attended = (state[2] / state[1][:, :, None]).astype(jnp.bfloat16).reshape(count, heads * HD)
    hidden_part = w_gate.shape[2]
    packed = jnp.concatenate([w_gate[0], w_up[0], w_down[0].T], axis=1)
    across = lax.ppermute(packed, "tp", [(source, source ^ 2) for source in range(tp_count)])
    sibling = [(source, source ^ 1) for source in range(tp_count)]
    weight_parts = [packed, across, lax.ppermute(packed, "tp", sibling), lax.ppermute(across, "tp", sibling)]
    projected = jnp.dot(attended, w_out, preferred_element_type=jnp.float32)
    experts = lax.axis_size("seq") * w_gate.shape[0]
    choose = expert_picks.shape[1]
    capacity = count * choose * 5 // (4 * experts)
    share = capacity // tp_count
    slots = experts * share
    onehot = (expert_picks[:, :, None] == jnp.arange(experts, dtype=jnp.int32)[None, None, :]).astype(
        jnp.float32
    )
    earlier = (
        jnp.arange(count, dtype=jnp.int32)[:, None] > jnp.arange(count, dtype=jnp.int32)[None, :]
    ).astype(jnp.bfloat16)
    before = jnp.dot(
        earlier, jnp.sum(onehot, axis=1).astype(jnp.bfloat16), preferred_element_type=jnp.float32
    )
    ranks = jnp.sum(before[:, None, :] * onehot, axis=2).astype(jnp.int32)
    owner = ranks // share
    slot = expert_picks * share + ranks % share
    mine_slot = jnp.where(owner == tp_index, slot, slots)
    slot_range = jnp.arange(slots, dtype=jnp.int32)
    placing = jnp.sum(
        (mine_slot[:, :, None] == slot_range[None, None, :]).astype(jnp.bfloat16), axis=1
    ).T
    part_width = tokens.shape[1] // tp_count
    summed = lax.psum(projected.astype(jnp.bfloat16), "tp")
    summed, weight_parts = lax.optimization_barrier((summed, weight_parts))
    summed = summed.astype(jnp.float32)
    residual = tokens.astype(jnp.float32) + summed
    mixed_in = row_norm(residual, ffn_gain).astype(jnp.bfloat16)
    columns = mixed_in.shape[1]
    rows = jnp.dot(placing, mixed_in, preferred_element_type=jnp.float32).astype(jnp.bfloat16)
    arrived = lax.all_to_all(rows, "seq", split_axis=0, concat_axis=0, tiled=True)
    gate_full = jnp.concatenate([part[:, :hidden_part] for part in weight_parts], axis=1)
    up_full = jnp.concatenate([part[:, hidden_part : 2 * hidden_part] for part in weight_parts], axis=1)
    down_full = jnp.concatenate([part[:, 2 * hidden_part :] for part in weight_parts], axis=1).T
    gate_part = jnp.dot(arrived, gate_full, preferred_element_type=jnp.float32)
    up_part = jnp.dot(arrived, up_full, preferred_element_type=jnp.float32)
    hidden = (jax.nn.relu(gate_part) * up_part).astype(jnp.bfloat16)
    expert_out = jnp.dot(hidden, down_full, preferred_element_type=jnp.float32).astype(jnp.bfloat16)
    sources = lax.axis_size("seq")
    outgoing = (
        expert_out.reshape(sources, share, tp_count, part_width)
        .transpose(0, 2, 1, 3)
        .reshape(sources * tp_count * share, part_width)
    )
    mine = lax.all_to_all(outgoing, ("seq", "tp"), split_axis=0, concat_axis=0, tiled=True)
    residual_part = lax.dynamic_slice_in_dim(residual, tp_index * part_width, part_width, 1)
    every_slot = jnp.arange(experts * capacity, dtype=jnp.int32)
    picked = (expert_picks * capacity + ranks)[:, :, None] == every_slot[None, None, :]
    scales = jnp.sum(jnp.where(picked, gate_weights[:, :, None], 0.0), axis=1)
    high = scales.astype(jnp.bfloat16)
    low = (scales - high.astype(jnp.float32)).astype(jnp.bfloat16)
    mixture = jnp.dot(high, mine, preferred_element_type=jnp.float32) + jnp.dot(
        low, mine, preferred_element_type=jnp.float32
    )
    layer_out = (residual_part + mixture).astype(jnp.bfloat16)
    return (layer_out, kv_pages)


def solution(mesh):
    placed = (
        P("seq", None),
        P("seq"),
        P(),
        P(None, "tp"),
        P(),
        P("tp", None),
        P(),
        P("seq", None, "tp"),
        P("seq", None, "tp"),
        P("seq", "tp", None),
        P("seq", None),
        P("seq", None),
        P("seq"),
    )
    return jax.shard_map(
        per_device,
        mesh=mesh,
        in_specs=placed,
        out_specs=(P("seq", "tp"), P("seq", None, "tp")),
        check_vma=False,
    )
```

```python
import jax
import jax.numpy as jnp
from jax import lax
from jax.sharding import PartitionSpec as P

HQ = 12
HK = 2
HD = 128


EPSILON = 1e-06
NEGATIVE = -1e30


def shifted(value, axis, steps):
    count = lax.axis_size(axis)
    leading, last = (max(0, -steps), min(count, count - steps))
    return lax.ppermute(value, axis, [(source, source + steps) for source in range(leading, last)])


def row_norm(values, gain):
    values = values.astype(jnp.float32)
    factor = lax.rsqrt(jnp.mean(values * values, axis=-1, keepdims=True) + EPSILON)
    return values * factor * gain


def attend_block(carry, queries, key_block, value_block, allowed):
    running, total, accum = carry
    scores = jnp.einsum(
        "qhd,kd->qhk", queries, key_block, preferred_element_type=jnp.float32
    ) * HD ** (-0.5)
    open_mask = allowed[:, None, :]
    highest = jnp.max(jnp.where(open_mask, scores, NEGATIVE), axis=2)
    renewed = jnp.maximum(running, highest)
    weights = jnp.where(open_mask, jnp.exp(scores - renewed[:, :, None]), 0.0)
    factor = jnp.exp(running - renewed)
    total = total * factor + jnp.sum(weights, axis=2)
    accum = accum * factor[:, :, None] + jnp.einsum(
        "qhk,kd->qhd", weights.astype(jnp.bfloat16), value_block, preferred_element_type=jnp.float32
    )
    return (renewed, total, accum)


def per_device(
    tokens,
    segment_ids,
    attn_gain,
    w_query,
    w_kv,
    w_out,
    ffn_gain,
    w_gate,
    w_up,
    w_down,
    expert_picks,
    gate_weights,
    page_table,
):
    count = tokens.shape[0]
    seq_index = lax.axis_index("seq")
    tp_index = lax.axis_index("tp")
    tp_count = lax.axis_size("tp")
    normed = row_norm(tokens, attn_gain).astype(jnp.bfloat16)
    queries = jnp.dot(normed, w_query, preferred_element_type=jnp.float32).astype(jnp.bfloat16)
    keyval = jnp.dot(normed, w_kv, preferred_element_type=jnp.float32).astype(jnp.bfloat16)
    cache_width = keyval.shape[1] // tp_count
    cache_columns = lax.dynamic_slice_in_dim(keyval, tp_index * cache_width, cache_width, 1)
    page_rows = page_table.shape[0]
    page_length = count // page_rows
    local_pages = page_table - seq_index * page_rows
    kv_pages = (
        jnp.zeros((page_rows, page_length, cache_width), jnp.bfloat16)
        .at[local_pages]
        .set(cache_columns.reshape(page_rows, page_length, cache_width))
    )
    heads = queries.shape[1] // HD
    group = tp_index * heads // (HQ // HK)
    key_head = lax.dynamic_slice_in_dim(keyval, group * HD, HD, 1)
    value_head = lax.dynamic_slice_in_dim(keyval, (HK + group) * HD, HD, 1)
    query_heads = queries.reshape(count, heads, HD)
    query_index = seq_index * count + jnp.arange(count, dtype=jnp.int32)
    width = 2 * HD
    code_rows = 2 * count // width
    code = jnp.stack([segment_ids // 256, segment_ids % 256]).astype(jnp.bfloat16).reshape(code_rows, width)
    code = jnp.concatenate([code, jnp.zeros((16 - code_rows % 16, width), jnp.bfloat16)], axis=0)
    own_piece = jnp.concatenate([jnp.concatenate([key_head, value_head], axis=1), code], axis=0)
    reach_steps = lax.axis_size("seq") // 4
    pieces = [own_piece] + [shifted(own_piece, "seq", number) for number in range(1, reach_steps + 1)]

    halves = 2
    half = count // halves

    def visit(carry, piece, number, rows):
        start = (seq_index - number) * count
        key_index = start + jnp.arange(count, dtype=jnp.int32)
        coded = piece[count : count + code_rows].reshape(2, count).astype(jnp.int32)
        segment_piece = coded[0] * 256 + coded[1]
        allowed = (
            (segment_piece[None, :] == segment_ids[rows, None])
            & (key_index[None, :] <= query_index[rows, None])
            & (key_index[None, :] >= 0)
        )
        return attend_block(carry, query_heads[rows], piece[:count, :HD], piece[:count, HD:], allowed)

    summed_parts = []
    for part in range(halves):
        rows = slice(part * half, (part + 1) * half)
        state = (
            jnp.full((half, heads), NEGATIVE, jnp.float32),
            jnp.zeros((half, heads), jnp.float32),
            jnp.zeros((half, heads, HD), jnp.float32),
        )
        for number, piece in enumerate(pieces):
            state = visit(state, piece, number, rows)
        attended = (state[2] / state[1][:, :, None]).astype(jnp.bfloat16).reshape(half, heads * HD)
        projected = jnp.dot(attended, w_out, preferred_element_type=jnp.float32).astype(jnp.bfloat16)
        if summed_parts:
            summed_parts[-1], projected = lax.optimization_barrier((summed_parts[-1], projected))
        summed_parts.append(lax.psum(projected, "tp"))
    hidden_part = w_gate.shape[2]
    packed = jnp.concatenate([w_gate[0], w_up[0], w_down[0].T], axis=1)
    across = lax.ppermute(packed, "tp", [(source, source ^ 2) for source in range(tp_count)])
    sibling = [(source, source ^ 1) for source in range(tp_count)]
    weight_parts = [packed, across, lax.ppermute(packed, "tp", sibling), lax.ppermute(across, "tp", sibling)]
    experts = lax.axis_size("seq") * w_gate.shape[0]
    choose = expert_picks.shape[1]
    capacity = count * choose * 5 // (4 * experts)
    share = capacity // tp_count
    slots = experts * share
    onehot = (expert_picks[:, :, None] == jnp.arange(experts, dtype=jnp.int32)[None, None, :]).astype(
        jnp.float32
    )
    earlier = (
        jnp.arange(count, dtype=jnp.int32)[:, None] > jnp.arange(count, dtype=jnp.int32)[None, :]
    ).astype(jnp.bfloat16)
    before = jnp.dot(
        earlier, jnp.sum(onehot, axis=1).astype(jnp.bfloat16), preferred_element_type=jnp.float32
    )
    ranks = jnp.sum(before[:, None, :] * onehot, axis=2).astype(jnp.int32)
    owner = ranks // share
    slot = expert_picks * share + ranks % share
    mine_slot = jnp.where(owner == tp_index, slot, slots)
    slot_range = jnp.arange(slots, dtype=jnp.int32)
    placing = jnp.sum(
        (mine_slot[:, :, None] == slot_range[None, None, :]).astype(jnp.bfloat16), axis=1
    ).T
    part_width = tokens.shape[1] // tp_count
    summed = jnp.concatenate(summed_parts, axis=0)
    summed, weight_parts = lax.optimization_barrier((summed, weight_parts))
    summed = summed.astype(jnp.float32)
    residual = tokens.astype(jnp.float32) + summed
    mixed_in = row_norm(residual, ffn_gain).astype(jnp.bfloat16)
    columns = mixed_in.shape[1]
    rows = jnp.dot(placing, mixed_in, preferred_element_type=jnp.float32).astype(jnp.bfloat16)
    arrived = lax.all_to_all(rows, "seq", split_axis=0, concat_axis=0, tiled=True)
    gate_full = jnp.concatenate([part[:, :hidden_part] for part in weight_parts], axis=1)
    up_full = jnp.concatenate([part[:, hidden_part : 2 * hidden_part] for part in weight_parts], axis=1)
    down_full = jnp.concatenate([part[:, 2 * hidden_part :] for part in weight_parts], axis=1).T
    gate_part = jnp.dot(arrived, gate_full, preferred_element_type=jnp.float32)
    up_part = jnp.dot(arrived, up_full, preferred_element_type=jnp.float32)
    hidden = (jax.nn.relu(gate_part) * up_part).astype(jnp.bfloat16)
    expert_out = jnp.dot(hidden, down_full, preferred_element_type=jnp.float32).astype(jnp.bfloat16)
    sources = lax.axis_size("seq")
    outgoing = (
        expert_out.reshape(sources, share, tp_count, part_width)
        .transpose(0, 2, 1, 3)
        .reshape(sources * tp_count * share, part_width)
    )
    mine = lax.all_to_all(outgoing, ("seq", "tp"), split_axis=0, concat_axis=0, tiled=True)
    residual_part = lax.dynamic_slice_in_dim(residual, tp_index * part_width, part_width, 1)
    every_slot = jnp.arange(experts * capacity, dtype=jnp.int32)
    picked = (expert_picks * capacity + ranks)[:, :, None] == every_slot[None, None, :]
    scales = jnp.sum(jnp.where(picked, gate_weights[:, :, None], 0.0), axis=1)
    high = scales.astype(jnp.bfloat16)
    low = (scales - high.astype(jnp.float32)).astype(jnp.bfloat16)
    mixture = jnp.dot(high, mine, preferred_element_type=jnp.float32) + jnp.dot(
        low, mine, preferred_element_type=jnp.float32
    )
    layer_out = (residual_part + mixture).astype(jnp.bfloat16)
    return (layer_out, kv_pages)


def solution(mesh):
    placed = (
        P("seq", None),
        P("seq"),
        P(),
        P(None, "tp"),
        P(),
        P("tp", None),
        P(),
        P("seq", None, "tp"),
        P("seq", None, "tp"),
        P("seq", "tp", None),
        P("seq", None),
        P("seq", None),
        P("seq"),
    )
    return jax.shard_map(
        per_device,
        mesh=mesh,
        in_specs=placed,
        out_specs=(P("seq", "tp"), P("seq", None, "tp")),
        check_vma=False,
    )
```

```python
import jax
import jax.numpy as jnp
from jax import lax
from jax.sharding import PartitionSpec as P

HQ = 12
HK = 2
HD = 128


EPSILON = 1e-06
NEGATIVE = -1e30


def shifted(value, axis, steps):
    count = lax.axis_size(axis)
    leading, last = (max(0, -steps), min(count, count - steps))
    return lax.ppermute(value, axis, [(source, source + steps) for source in range(leading, last)])


def row_norm(values, gain):
    values = values.astype(jnp.float32)
    factor = lax.rsqrt(jnp.mean(values * values, axis=-1, keepdims=True) + EPSILON)
    return values * factor * gain


def attend_block(carry, queries, key_block, value_block, allowed):
    running, total, accum = carry
    scores = jnp.einsum(
        "qhd,kd->qhk", queries, key_block, preferred_element_type=jnp.float32
    ) * HD ** (-0.5)
    open_mask = allowed[:, None, :]
    highest = jnp.max(jnp.where(open_mask, scores, NEGATIVE), axis=2)
    renewed = jnp.maximum(running, highest)
    weights = jnp.where(open_mask, jnp.exp(scores - renewed[:, :, None]), 0.0)
    factor = jnp.exp(running - renewed)
    total = total * factor + jnp.sum(weights, axis=2)
    accum = accum * factor[:, :, None] + jnp.einsum(
        "qhk,kd->qhd", weights.astype(jnp.bfloat16), value_block, preferred_element_type=jnp.float32
    )
    return (renewed, total, accum)


def per_device(
    tokens,
    segment_ids,
    attn_gain,
    w_query,
    w_kv,
    w_out,
    ffn_gain,
    w_gate,
    w_up,
    w_down,
    expert_picks,
    gate_weights,
    page_table,
):
    count = tokens.shape[0]
    seq_index = lax.axis_index("seq")
    tp_index = lax.axis_index("tp")
    tp_count = lax.axis_size("tp")
    normed = row_norm(tokens, attn_gain).astype(jnp.bfloat16)
    queries = jnp.dot(normed, w_query, preferred_element_type=jnp.float32).astype(jnp.bfloat16)
    keyval = jnp.dot(normed, w_kv, preferred_element_type=jnp.float32).astype(jnp.bfloat16)
    cache_width = keyval.shape[1] // tp_count
    cache_columns = lax.dynamic_slice_in_dim(keyval, tp_index * cache_width, cache_width, 1)
    page_rows = page_table.shape[0]
    page_length = count // page_rows
    local_pages = page_table - seq_index * page_rows
    kv_pages = (
        jnp.zeros((page_rows, page_length, cache_width), jnp.bfloat16)
        .at[local_pages]
        .set(cache_columns.reshape(page_rows, page_length, cache_width))
    )
    heads = queries.shape[1] // HD
    group = tp_index * heads // (HQ // HK)
    key_head = lax.dynamic_slice_in_dim(keyval, group * HD, HD, 1)
    value_head = lax.dynamic_slice_in_dim(keyval, (HK + group) * HD, HD, 1)
    query_heads = queries.reshape(count, heads, HD)
    query_index = seq_index * count + jnp.arange(count, dtype=jnp.int32)
    width = 2 * HD
    code_rows = 2 * count // width
    code = jnp.stack([segment_ids // 256, segment_ids % 256]).astype(jnp.bfloat16).reshape(code_rows, width)
    code = jnp.concatenate([code, jnp.zeros((16 - code_rows % 16, width), jnp.bfloat16)], axis=0)
    own_piece = jnp.concatenate([jnp.concatenate([key_head, value_head], axis=1), code], axis=0)
    reach_steps = lax.axis_size("seq") // 4
    seq_count = lax.axis_size("seq")
    rounds = reach_steps // 2
    core = tp_index % 2
    fetched = []
    for number in range(1, rounds + 1):
        pairs = []
        for source_seq in range(seq_count):
            for lane in range(tp_count):
                target_seq = source_seq + number + rounds * (lane % 2)
                if target_seq < seq_count:
                    pairs.append((source_seq * tp_count + lane, target_seq * tp_count + lane))
        fetched.append(lax.ppermute(own_piece, ("seq", "tp"), pairs))
    swapped = lax.ppermute(jnp.stack(fetched), "tp", [(lane, lane ^ 1) for lane in range(tp_count)])
    pieces = [(own_piece, 0)]
    pieces += [(piece, number + 1 + rounds * core) for number, piece in enumerate(fetched)]
    pieces += [(swapped[number], number + 1 + rounds * (1 - core)) for number in range(rounds)]

    def visit(carry, piece, number):
        start = (seq_index - number) * count
        key_index = start + jnp.arange(count, dtype=jnp.int32)
        coded = piece[count : count + code_rows].reshape(2, count).astype(jnp.int32)
        segment_piece = coded[0] * 256 + coded[1]
        allowed = (
            (segment_piece[None, :] == segment_ids[:, None])
            & (key_index[None, :] <= query_index[:, None])
            & (key_index[None, :] >= 0)
        )
        return attend_block(carry, query_heads, piece[:count, :HD], piece[:count, HD:], allowed)

    state = (
        jnp.full((count, heads), NEGATIVE, jnp.float32),
        jnp.zeros((count, heads), jnp.float32),
        jnp.zeros((count, heads, HD), jnp.float32),
    )
    for piece, number in pieces:
        state = visit(state, piece, number)
    attended = (state[2] / state[1][:, :, None]).astype(jnp.bfloat16).reshape(count, heads * HD)
    hidden_part = w_gate.shape[2]
    packed = jnp.concatenate([w_gate[0], w_up[0], w_down[0].T], axis=1)
    across = lax.ppermute(packed, "tp", [(source, source ^ 2) for source in range(tp_count)])
    sibling = [(source, source ^ 1) for source in range(tp_count)]
    weight_parts = [packed, across, lax.ppermute(packed, "tp", sibling), lax.ppermute(across, "tp", sibling)]
    projected = jnp.dot(attended, w_out, preferred_element_type=jnp.float32)
    experts = lax.axis_size("seq") * w_gate.shape[0]
    choose = expert_picks.shape[1]
    capacity = count * choose * 5 // (4 * experts)
    share = capacity // tp_count
    slots = experts * share
    onehot = (expert_picks[:, :, None] == jnp.arange(experts, dtype=jnp.int32)[None, None, :]).astype(
        jnp.float32
    )
    earlier = (
        jnp.arange(count, dtype=jnp.int32)[:, None] > jnp.arange(count, dtype=jnp.int32)[None, :]
    ).astype(jnp.bfloat16)
    before = jnp.dot(
        earlier, jnp.sum(onehot, axis=1).astype(jnp.bfloat16), preferred_element_type=jnp.float32
    )
    ranks = jnp.sum(before[:, None, :] * onehot, axis=2).astype(jnp.int32)
    owner = ranks // share
    slot = expert_picks * share + ranks % share
    mine_slot = jnp.where(owner == tp_index, slot, slots)
    slot_range = jnp.arange(slots, dtype=jnp.int32)
    placing = jnp.sum(
        (mine_slot[:, :, None] == slot_range[None, None, :]).astype(jnp.bfloat16), axis=1
    ).T
    part_width = tokens.shape[1] // tp_count
    summed = lax.psum(projected.astype(jnp.bfloat16), "tp")
    summed, weight_parts = lax.optimization_barrier((summed, weight_parts))
    summed = summed.astype(jnp.float32)
    residual = tokens.astype(jnp.float32) + summed
    mixed_in = row_norm(residual, ffn_gain).astype(jnp.bfloat16)
    columns = mixed_in.shape[1]
    rows = jnp.dot(placing, mixed_in, preferred_element_type=jnp.float32).astype(jnp.bfloat16)
    arrived = lax.all_to_all(rows, "seq", split_axis=0, concat_axis=0, tiled=True)
    gate_full = jnp.concatenate([part[:, :hidden_part] for part in weight_parts], axis=1)
    up_full = jnp.concatenate([part[:, hidden_part : 2 * hidden_part] for part in weight_parts], axis=1)
    down_full = jnp.concatenate([part[:, 2 * hidden_part :] for part in weight_parts], axis=1).T
    gate_part = jnp.dot(arrived, gate_full, preferred_element_type=jnp.float32)
    up_part = jnp.dot(arrived, up_full, preferred_element_type=jnp.float32)
    hidden = (jax.nn.relu(gate_part) * up_part).astype(jnp.bfloat16)
    expert_out = jnp.dot(hidden, down_full, preferred_element_type=jnp.float32).astype(jnp.bfloat16)
    sources = lax.axis_size("seq")
    outgoing = (
        expert_out.reshape(sources, share, tp_count, part_width)
        .transpose(0, 2, 1, 3)
        .reshape(sources * tp_count * share, part_width)
    )
    mine = lax.all_to_all(outgoing, ("seq", "tp"), split_axis=0, concat_axis=0, tiled=True)
    residual_part = lax.dynamic_slice_in_dim(residual, tp_index * part_width, part_width, 1)
    every_slot = jnp.arange(experts * capacity, dtype=jnp.int32)
    picked = (expert_picks * capacity + ranks)[:, :, None] == every_slot[None, None, :]
    scales = jnp.sum(jnp.where(picked, gate_weights[:, :, None], 0.0), axis=1)
    high = scales.astype(jnp.bfloat16)
    low = (scales - high.astype(jnp.float32)).astype(jnp.bfloat16)
    mixture = jnp.dot(high, mine, preferred_element_type=jnp.float32) + jnp.dot(
        low, mine, preferred_element_type=jnp.float32
    )
    layer_out = (residual_part + mixture).astype(jnp.bfloat16)
    return (layer_out, kv_pages)


def solution(mesh):
    placed = (
        P("seq", None),
        P("seq"),
        P(),
        P(None, "tp"),
        P(),
        P("tp", None),
        P(),
        P("seq", None, "tp"),
        P("seq", None, "tp"),
        P("seq", "tp", None),
        P("seq", None),
        P("seq", None),
        P("seq"),
    )
    return jax.shard_map(
        per_device,
        mesh=mesh,
        in_specs=placed,
        out_specs=(P("seq", "tp"), P("seq", None, "tp")),
        check_vma=False,
    )
```

```python
import jax
import jax.numpy as jnp
from jax import lax
from jax.sharding import PartitionSpec as P

HQ = 12
HK = 2
HD = 128


EPSILON = 1e-06
NEGATIVE = -1e30


def shifted(value, axis, steps):
    count = lax.axis_size(axis)
    leading, last = (max(0, -steps), min(count, count - steps))
    return lax.ppermute(value, axis, [(source, source + steps) for source in range(leading, last)])


def row_norm(values, gain):
    values = values.astype(jnp.float32)
    factor = lax.rsqrt(jnp.mean(values * values, axis=-1, keepdims=True) + EPSILON)
    return values * factor * gain


def attend_block(carry, queries, key_block, value_block, allowed):
    running, total, accum = carry
    scores = jnp.einsum(
        "qhd,kd->qhk", queries, key_block, preferred_element_type=jnp.float32
    ) * HD ** (-0.5)
    open_mask = allowed[:, None, :]
    highest = jnp.max(jnp.where(open_mask, scores, NEGATIVE), axis=2)
    renewed = jnp.maximum(running, highest)
    weights = jnp.where(open_mask, jnp.exp(scores - renewed[:, :, None]), 0.0)
    factor = jnp.exp(running - renewed)
    total = total * factor + jnp.sum(weights, axis=2)
    accum = accum * factor[:, :, None] + jnp.einsum(
        "qhk,kd->qhd", weights.astype(jnp.bfloat16), value_block, preferred_element_type=jnp.float32
    )
    return (renewed, total, accum)


def per_device(
    tokens,
    segment_ids,
    attn_gain,
    w_query,
    w_kv,
    w_out,
    ffn_gain,
    w_gate,
    w_up,
    w_down,
    expert_picks,
    gate_weights,
    page_table,
):
    count = tokens.shape[0]
    seq_index = lax.axis_index("seq")
    tp_index = lax.axis_index("tp")
    tp_count = lax.axis_size("tp")
    normed = row_norm(tokens, attn_gain).astype(jnp.bfloat16)
    queries = jnp.dot(normed, w_query, preferred_element_type=jnp.float32).astype(jnp.bfloat16)
    keyval = jnp.dot(normed, w_kv, preferred_element_type=jnp.float32).astype(jnp.bfloat16)
    cache_width = keyval.shape[1] // tp_count
    cache_columns = lax.dynamic_slice_in_dim(keyval, tp_index * cache_width, cache_width, 1)
    page_rows = page_table.shape[0]
    page_length = count // page_rows
    local_pages = page_table - seq_index * page_rows
    kv_pages = (
        jnp.zeros((page_rows, page_length, cache_width), jnp.bfloat16)
        .at[local_pages]
        .set(cache_columns.reshape(page_rows, page_length, cache_width))
    )
    heads = queries.shape[1] // HD
    group = tp_index * heads // (HQ // HK)
    key_head = lax.dynamic_slice_in_dim(keyval, group * HD, HD, 1)
    value_head = lax.dynamic_slice_in_dim(keyval, (HK + group) * HD, HD, 1)
    query_heads = queries.reshape(count, heads, HD)
    query_index = seq_index * count + jnp.arange(count, dtype=jnp.int32)
    width = 2 * HD
    code_rows = 2 * count // width
    code = jnp.stack([segment_ids // 256, segment_ids % 256]).astype(jnp.bfloat16).reshape(code_rows, width)
    code = jnp.concatenate([code, jnp.zeros((16 - code_rows % 16, width), jnp.bfloat16)], axis=0)
    own_piece = jnp.concatenate([jnp.concatenate([key_head, value_head], axis=1), code], axis=0)
    reach_steps = lax.axis_size("seq") // 4
    seq_count = lax.axis_size("seq")
    rounds = reach_steps // 2
    core = tp_index % 2
    fetched = []
    for number in range(1, rounds + 1):
        pairs = []
        for source_seq in range(seq_count):
            for lane in range(tp_count):
                target_seq = source_seq + number + rounds * (lane % 2)
                if target_seq < seq_count:
                    pairs.append((source_seq * tp_count + lane, target_seq * tp_count + lane))
        fetched.append(lax.ppermute(own_piece, ("seq", "tp"), pairs))
    swapped = lax.ppermute(jnp.stack(fetched), "tp", [(lane, lane ^ 1) for lane in range(tp_count)])
    pieces = [(own_piece, 0)]
    pieces += [(piece, number + 1 + rounds * core) for number, piece in enumerate(fetched)]
    pieces += [(swapped[number], number + 1 + rounds * (1 - core)) for number in range(rounds)]

    def visit(carry, piece, number):
        start = (seq_index - number) * count
        key_index = start + jnp.arange(count, dtype=jnp.int32)
        coded = piece[count : count + code_rows].reshape(2, count).astype(jnp.int32)
        segment_piece = coded[0] * 256 + coded[1]
        allowed = (
            (segment_piece[None, :] == segment_ids[:, None])
            & (key_index[None, :] <= query_index[:, None])
            & (key_index[None, :] >= 0)
        )
        return attend_block(carry, query_heads, piece[:count, :HD], piece[:count, HD:], allowed)

    state = (
        jnp.full((count, heads), NEGATIVE, jnp.float32),
        jnp.zeros((count, heads), jnp.float32),
        jnp.zeros((count, heads, HD), jnp.float32),
    )
    for piece, number in pieces:
        state = visit(state, piece, number)
    attended = (state[2] / state[1][:, :, None]).astype(jnp.bfloat16).reshape(count, heads * HD)
    hidden_part = w_gate.shape[2]
    packed = jnp.concatenate([w_gate[0], w_up[0], w_down[0].T], axis=1)
    across = lax.ppermute(packed, "tp", [(source, source ^ 2) for source in range(tp_count)])
    sibling = [(source, source ^ 1) for source in range(tp_count)]
    weight_parts = [packed, across, lax.ppermute(packed, "tp", sibling), lax.ppermute(across, "tp", sibling)]
    projected = jnp.dot(attended, w_out, preferred_element_type=jnp.float32)
    experts = lax.axis_size("seq") * w_gate.shape[0]
    choose = expert_picks.shape[1]
    capacity = count * choose * 5 // (4 * experts)
    share = capacity // tp_count
    slots = experts * share
    onehot = (expert_picks[:, :, None] == jnp.arange(experts, dtype=jnp.int32)[None, None, :]).astype(
        jnp.float32
    )
    earlier = (
        jnp.arange(count, dtype=jnp.int32)[:, None] > jnp.arange(count, dtype=jnp.int32)[None, :]
    ).astype(jnp.bfloat16)
    before = jnp.dot(
        earlier, jnp.sum(onehot, axis=1).astype(jnp.bfloat16), preferred_element_type=jnp.float32
    )
    ranks = jnp.sum(before[:, None, :] * onehot, axis=2).astype(jnp.int32)
    owner = ranks // share
    slot = expert_picks * share + ranks % share
    mine_slot = jnp.where(owner == tp_index, slot, slots)
    slot_range = jnp.arange(slots, dtype=jnp.int32)
    placing = jnp.sum(
        (mine_slot[:, :, None] == slot_range[None, None, :]).astype(jnp.bfloat16), axis=1
    ).T
    part_width = tokens.shape[1] // tp_count
    sibling_sum = lax.ppermute(projected.astype(jnp.bfloat16), "tp", sibling)
    chip_sum = projected + sibling_sum.astype(jnp.float32)
    half_width = chip_sum.shape[1] // 2
    own_half = lax.dynamic_slice_in_dim(chip_sum, core * half_width, half_width, 1)
    partner = [(lane, lane ^ 2) for lane in range(tp_count)]
    own_half = own_half + lax.ppermute(own_half.astype(jnp.bfloat16), "tp", partner).astype(jnp.float32)
    other_half = lax.ppermute(own_half.astype(jnp.bfloat16), "tp", sibling).astype(jnp.float32)
    summed = jnp.where(
        core == 0,
        jnp.concatenate([own_half, other_half], axis=1),
        jnp.concatenate([other_half, own_half], axis=1),
    )
    summed, weight_parts = lax.optimization_barrier((summed, weight_parts))
    residual = tokens.astype(jnp.float32) + summed
    mixed_in = row_norm(residual, ffn_gain).astype(jnp.bfloat16)
    columns = mixed_in.shape[1]
    rows = jnp.dot(placing, mixed_in, preferred_element_type=jnp.float32).astype(jnp.bfloat16)
    arrived = lax.all_to_all(rows, "seq", split_axis=0, concat_axis=0, tiled=True)
    gate_full = jnp.concatenate([part[:, :hidden_part] for part in weight_parts], axis=1)
    up_full = jnp.concatenate([part[:, hidden_part : 2 * hidden_part] for part in weight_parts], axis=1)
    down_full = jnp.concatenate([part[:, 2 * hidden_part :] for part in weight_parts], axis=1).T
    gate_part = jnp.dot(arrived, gate_full, preferred_element_type=jnp.float32)
    up_part = jnp.dot(arrived, up_full, preferred_element_type=jnp.float32)
    hidden = (jax.nn.relu(gate_part) * up_part).astype(jnp.bfloat16)
    expert_out = jnp.dot(hidden, down_full, preferred_element_type=jnp.float32).astype(jnp.bfloat16)
    sources = lax.axis_size("seq")
    outgoing = (
        expert_out.reshape(sources, share, tp_count, part_width)
        .transpose(0, 2, 1, 3)
        .reshape(sources * tp_count * share, part_width)
    )
    mine = lax.all_to_all(outgoing, ("seq", "tp"), split_axis=0, concat_axis=0, tiled=True)
    residual_part = lax.dynamic_slice_in_dim(residual, tp_index * part_width, part_width, 1)
    every_slot = jnp.arange(experts * capacity, dtype=jnp.int32)
    picked = (expert_picks * capacity + ranks)[:, :, None] == every_slot[None, None, :]
    scales = jnp.sum(jnp.where(picked, gate_weights[:, :, None], 0.0), axis=1)
    high = scales.astype(jnp.bfloat16)
    low = (scales - high.astype(jnp.float32)).astype(jnp.bfloat16)
    mixture = jnp.dot(high, mine, preferred_element_type=jnp.float32) + jnp.dot(
        low, mine, preferred_element_type=jnp.float32
    )
    layer_out = (residual_part + mixture).astype(jnp.bfloat16)
    return (layer_out, kv_pages)


def solution(mesh):
    placed = (
        P("seq", None),
        P("seq"),
        P(),
        P(None, "tp"),
        P(),
        P("tp", None),
        P(),
        P("seq", None, "tp"),
        P("seq", None, "tp"),
        P("seq", "tp", None),
        P("seq", None),
        P("seq", None),
        P("seq"),
    )
    return jax.shard_map(
        per_device,
        mesh=mesh,
        in_specs=placed,
        out_specs=(P("seq", "tp"), P("seq", None, "tp")),
        check_vma=False,
    )
```

```python
import jax
import jax.numpy as jnp
from jax import lax
from jax.sharding import PartitionSpec as P

HQ = 12
HK = 2
HD = 128


EPSILON = 1e-06
NEGATIVE = -1e30


def shifted(value, axis, steps):
    count = lax.axis_size(axis)
    leading, last = (max(0, -steps), min(count, count - steps))
    return lax.ppermute(value, axis, [(source, source + steps) for source in range(leading, last)])


def row_norm(values, gain):
    values = values.astype(jnp.float32)
    factor = lax.rsqrt(jnp.mean(values * values, axis=-1, keepdims=True) + EPSILON)
    return values * factor * gain


def attend_block(carry, queries, key_block, value_block, allowed):
    running, total, accum = carry
    scores = jnp.einsum(
        "qhd,kd->qhk", queries, key_block, preferred_element_type=jnp.float32
    ) * HD ** (-0.5)
    open_mask = allowed[:, None, :]
    highest = jnp.max(jnp.where(open_mask, scores, NEGATIVE), axis=2)
    renewed = jnp.maximum(running, highest)
    weights = jnp.where(open_mask, jnp.exp(scores - renewed[:, :, None]), 0.0)
    factor = jnp.exp(running - renewed)
    total = total * factor + jnp.sum(weights, axis=2)
    accum = accum * factor[:, :, None] + jnp.einsum(
        "qhk,kd->qhd", weights.astype(jnp.bfloat16), value_block, preferred_element_type=jnp.float32
    )
    return (renewed, total, accum)


def per_device(
    tokens,
    segment_ids,
    attn_gain,
    w_query,
    w_kv,
    w_out,
    ffn_gain,
    w_gate,
    w_up,
    w_down,
    expert_picks,
    gate_weights,
    page_table,
):
    count = tokens.shape[0]
    seq_index = lax.axis_index("seq")
    tp_index = lax.axis_index("tp")
    tp_count = lax.axis_size("tp")
    normed = row_norm(tokens, attn_gain).astype(jnp.bfloat16)
    queries = jnp.dot(normed, w_query, preferred_element_type=jnp.float32).astype(jnp.bfloat16)
    keyval = jnp.dot(normed, w_kv, preferred_element_type=jnp.float32).astype(jnp.bfloat16)
    cache_width = keyval.shape[1] // tp_count
    cache_columns = lax.dynamic_slice_in_dim(keyval, tp_index * cache_width, cache_width, 1)
    page_rows = page_table.shape[0]
    page_length = count // page_rows
    local_pages = page_table - seq_index * page_rows
    kv_pages = (
        jnp.zeros((page_rows, page_length, cache_width), jnp.bfloat16)
        .at[local_pages]
        .set(cache_columns.reshape(page_rows, page_length, cache_width))
    )
    heads = queries.shape[1] // HD
    group = tp_index * heads // (HQ // HK)
    key_head = lax.dynamic_slice_in_dim(keyval, group * HD, HD, 1)
    value_head = lax.dynamic_slice_in_dim(keyval, (HK + group) * HD, HD, 1)
    query_heads = queries.reshape(count, heads, HD)
    query_index = seq_index * count + jnp.arange(count, dtype=jnp.int32)
    width = 2 * HD
    code_rows = 2 * count // width
    code = jnp.stack([segment_ids // 256, segment_ids % 256]).astype(jnp.bfloat16).reshape(code_rows, width)
    code = jnp.concatenate([code, jnp.zeros((16 - code_rows % 16, width), jnp.bfloat16)], axis=0)
    own_piece = jnp.concatenate([jnp.concatenate([key_head, value_head], axis=1), code], axis=0)
    reach_steps = lax.axis_size("seq") // 4
    seq_count = lax.axis_size("seq")
    rounds = reach_steps // 2
    core = tp_index % 2
    fetched = []
    for number in range(1, rounds + 1):
        pairs = []
        for source_seq in range(seq_count):
            for lane in range(tp_count):
                target_seq = source_seq + number + rounds * (lane % 2)
                if target_seq < seq_count:
                    pairs.append((source_seq * tp_count + lane, target_seq * tp_count + lane))
        fetched.append(lax.ppermute(own_piece, ("seq", "tp"), pairs))
    swapped = lax.ppermute(jnp.stack(fetched), "tp", [(lane, lane ^ 1) for lane in range(tp_count)])
    pieces = [(own_piece, 0)]
    pieces += [(piece, number + 1 + rounds * core) for number, piece in enumerate(fetched)]
    pieces += [(swapped[number], number + 1 + rounds * (1 - core)) for number in range(rounds)]

    def visit(carry, piece, number):
        start = (seq_index - number) * count
        key_index = start + jnp.arange(count, dtype=jnp.int32)
        coded = piece[count : count + code_rows].reshape(2, count).astype(jnp.int32)
        segment_piece = coded[0] * 256 + coded[1]
        allowed = (
            (segment_piece[None, :] == segment_ids[:, None])
            & (key_index[None, :] <= query_index[:, None])
            & (key_index[None, :] >= 0)
        )
        return attend_block(carry, query_heads, piece[:count, :HD], piece[:count, HD:], allowed)

    state = (
        jnp.full((count, heads), NEGATIVE, jnp.float32),
        jnp.zeros((count, heads), jnp.float32),
        jnp.zeros((count, heads, HD), jnp.float32),
    )
    for piece, number in pieces:
        state = visit(state, piece, number)
    attended = (state[2] / state[1][:, :, None]).astype(jnp.bfloat16).reshape(count, heads * HD)
    hidden_part = w_gate.shape[2]
    packed = jnp.concatenate([w_gate[0], w_up[0], w_down[0].T], axis=1)
    across = lax.ppermute(packed, "tp", [(source, source ^ 2) for source in range(tp_count)])
    attended, across = lax.optimization_barrier((attended, across))
    sibling = [(source, source ^ 1) for source in range(tp_count)]
    weight_parts = [packed, across, lax.ppermute(packed, "tp", sibling), lax.ppermute(across, "tp", sibling)]
    projected = jnp.dot(attended, w_out, preferred_element_type=jnp.float32)
    experts = lax.axis_size("seq") * w_gate.shape[0]
    choose = expert_picks.shape[1]
    capacity = count * choose * 5 // (4 * experts)
    share = capacity // tp_count
    slots = experts * share
    onehot = (expert_picks[:, :, None] == jnp.arange(experts, dtype=jnp.int32)[None, None, :]).astype(
        jnp.float32
    )
    earlier = (
        jnp.arange(count, dtype=jnp.int32)[:, None] > jnp.arange(count, dtype=jnp.int32)[None, :]
    ).astype(jnp.bfloat16)
    before = jnp.dot(
        earlier, jnp.sum(onehot, axis=1).astype(jnp.bfloat16), preferred_element_type=jnp.float32
    )
    ranks = jnp.sum(before[:, None, :] * onehot, axis=2).astype(jnp.int32)
    owner = ranks // share
    slot = expert_picks * share + ranks % share
    mine_slot = jnp.where(owner == tp_index, slot, slots)
    slot_range = jnp.arange(slots, dtype=jnp.int32)
    placing = jnp.sum(
        (mine_slot[:, :, None] == slot_range[None, None, :]).astype(jnp.bfloat16), axis=1
    ).T
    part_width = tokens.shape[1] // tp_count
    sibling_sum = lax.ppermute(projected.astype(jnp.bfloat16), "tp", sibling)
    chip_sum = projected + sibling_sum.astype(jnp.float32)
    half_width = chip_sum.shape[1] // 2
    own_half = lax.dynamic_slice_in_dim(chip_sum, core * half_width, half_width, 1)
    partner = [(lane, lane ^ 2) for lane in range(tp_count)]
    own_half = own_half + lax.ppermute(own_half.astype(jnp.bfloat16), "tp", partner).astype(jnp.float32)
    other_half = lax.ppermute(own_half.astype(jnp.bfloat16), "tp", sibling).astype(jnp.float32)
    summed = jnp.where(
        core == 0,
        jnp.concatenate([own_half, other_half], axis=1),
        jnp.concatenate([other_half, own_half], axis=1),
    )
    summed, weight_parts = lax.optimization_barrier((summed, weight_parts))
    residual = tokens.astype(jnp.float32) + summed
    mixed_in = row_norm(residual, ffn_gain).astype(jnp.bfloat16)
    columns = mixed_in.shape[1]
    rows = jnp.dot(placing, mixed_in, preferred_element_type=jnp.float32).astype(jnp.bfloat16)
    arrived = lax.all_to_all(rows, "seq", split_axis=0, concat_axis=0, tiled=True)
    gate_full = jnp.concatenate([part[:, :hidden_part] for part in weight_parts], axis=1)
    up_full = jnp.concatenate([part[:, hidden_part : 2 * hidden_part] for part in weight_parts], axis=1)
    down_full = jnp.concatenate([part[:, 2 * hidden_part :] for part in weight_parts], axis=1).T
    gate_part = jnp.dot(arrived, gate_full, preferred_element_type=jnp.float32)
    up_part = jnp.dot(arrived, up_full, preferred_element_type=jnp.float32)
    hidden = (jax.nn.relu(gate_part) * up_part).astype(jnp.bfloat16)
    expert_out = jnp.dot(hidden, down_full, preferred_element_type=jnp.float32).astype(jnp.bfloat16)
    sources = lax.axis_size("seq")
    outgoing = (
        expert_out.reshape(sources, share, tp_count, part_width)
        .transpose(0, 2, 1, 3)
        .reshape(sources * tp_count * share, part_width)
    )
    mine = lax.all_to_all(outgoing, ("seq", "tp"), split_axis=0, concat_axis=0, tiled=True)
    residual_part = lax.dynamic_slice_in_dim(residual, tp_index * part_width, part_width, 1)
    every_slot = jnp.arange(experts * capacity, dtype=jnp.int32)
    picked = (expert_picks * capacity + ranks)[:, :, None] == every_slot[None, None, :]
    scales = jnp.sum(jnp.where(picked, gate_weights[:, :, None], 0.0), axis=1)
    high = scales.astype(jnp.bfloat16)
    low = (scales - high.astype(jnp.float32)).astype(jnp.bfloat16)
    mixture = jnp.dot(high, mine, preferred_element_type=jnp.float32) + jnp.dot(
        low, mine, preferred_element_type=jnp.float32
    )
    layer_out = (residual_part + mixture).astype(jnp.bfloat16)
    return (layer_out, kv_pages)


def solution(mesh):
    placed = (
        P("seq", None),
        P("seq"),
        P(),
        P(None, "tp"),
        P(),
        P("tp", None),
        P(),
        P("seq", None, "tp"),
        P("seq", None, "tp"),
        P("seq", "tp", None),
        P("seq", None),
        P("seq", None),
        P("seq"),
    )
    return jax.shard_map(
        per_device,
        mesh=mesh,
        in_specs=placed,
        out_specs=(P("seq", "tp"), P("seq", None, "tp")),
        check_vma=False,
    )
```

```python
import jax
import jax.numpy as jnp
from jax import lax
from jax.sharding import PartitionSpec as P

HQ = 12
HK = 2
HD = 128


EPSILON = 1e-06
NEGATIVE = -1e30


def shifted(value, axis, steps):
    count = lax.axis_size(axis)
    leading, last = (max(0, -steps), min(count, count - steps))
    return lax.ppermute(value, axis, [(source, source + steps) for source in range(leading, last)])


def row_norm(values, gain):
    values = values.astype(jnp.float32)
    factor = lax.rsqrt(jnp.mean(values * values, axis=-1, keepdims=True) + EPSILON)
    return values * factor * gain


def attend_block(carry, queries, key_block, value_block, allowed):
    running, total, accum = carry
    scores = jnp.einsum(
        "qhd,kd->qhk", queries, key_block, preferred_element_type=jnp.float32
    ) * HD ** (-0.5)
    open_mask = allowed[:, None, :]
    highest = jnp.max(jnp.where(open_mask, scores, NEGATIVE), axis=2)
    renewed = jnp.maximum(running, highest)
    weights = jnp.where(open_mask, jnp.exp(scores - renewed[:, :, None]), 0.0)
    factor = jnp.exp(running - renewed)
    total = total * factor + jnp.sum(weights, axis=2)
    accum = accum * factor[:, :, None] + jnp.einsum(
        "qhk,kd->qhd", weights.astype(jnp.bfloat16), value_block, preferred_element_type=jnp.float32
    )
    return (renewed, total, accum)


def per_device(
    tokens,
    segment_ids,
    attn_gain,
    w_query,
    w_kv,
    w_out,
    ffn_gain,
    w_gate,
    w_up,
    w_down,
    expert_picks,
    gate_weights,
    page_table,
):
    count = tokens.shape[0]
    seq_index = lax.axis_index("seq")
    tp_index = lax.axis_index("tp")
    tp_count = lax.axis_size("tp")
    normed = row_norm(tokens, attn_gain).astype(jnp.bfloat16)
    queries = jnp.dot(normed, w_query, preferred_element_type=jnp.float32).astype(jnp.bfloat16)
    keyval = jnp.dot(normed, w_kv, preferred_element_type=jnp.float32).astype(jnp.bfloat16)
    cache_width = keyval.shape[1] // tp_count
    cache_columns = lax.dynamic_slice_in_dim(keyval, tp_index * cache_width, cache_width, 1)
    page_rows = page_table.shape[0]
    page_length = count // page_rows
    local_pages = page_table - seq_index * page_rows
    kv_pages = (
        jnp.zeros((page_rows, page_length, cache_width), jnp.bfloat16)
        .at[local_pages]
        .set(cache_columns.reshape(page_rows, page_length, cache_width))
    )
    heads = queries.shape[1] // HD
    group = tp_index * heads // (HQ // HK)
    key_head = lax.dynamic_slice_in_dim(keyval, group * HD, HD, 1)
    value_head = lax.dynamic_slice_in_dim(keyval, (HK + group) * HD, HD, 1)
    query_heads = queries.reshape(count, heads, HD)
    query_index = seq_index * count + jnp.arange(count, dtype=jnp.int32)
    width = 2 * HD
    code_rows = 2 * count // width
    code = jnp.stack([segment_ids // 256, segment_ids % 256]).astype(jnp.bfloat16).reshape(code_rows, width)
    code = jnp.concatenate([code, jnp.zeros((16 - code_rows % 16, width), jnp.bfloat16)], axis=0)
    own_piece = jnp.concatenate([jnp.concatenate([key_head, value_head], axis=1), code], axis=0)
    reach_steps = lax.axis_size("seq") // 4
    seq_count = lax.axis_size("seq")
    rounds = reach_steps // 2
    core = tp_index % 2
    fetched = []
    for number in range(1, rounds + 1):
        pairs = []
        for source_seq in range(seq_count):
            for lane in range(tp_count):
                target_seq = source_seq + number + rounds * (lane % 2)
                if target_seq < seq_count:
                    pairs.append((source_seq * tp_count + lane, target_seq * tp_count + lane))
        fetched.append(lax.ppermute(own_piece, ("seq", "tp"), pairs))
    swapped = lax.ppermute(jnp.stack(fetched), "tp", [(lane, lane ^ 1) for lane in range(tp_count)])
    pieces = [(own_piece, 0)]
    pieces += [(piece, number + 1 + rounds * core) for number, piece in enumerate(fetched)]
    pieces += [(swapped[number], number + 1 + rounds * (1 - core)) for number in range(rounds)]

    def visit(carry, piece, number):
        start = (seq_index - number) * count
        key_index = start + jnp.arange(count, dtype=jnp.int32)
        coded = piece[count : count + code_rows].reshape(2, count).astype(jnp.int32)
        segment_piece = coded[0] * 256 + coded[1]
        allowed = (
            (segment_piece[None, :] == segment_ids[:, None])
            & (key_index[None, :] <= query_index[:, None])
            & (key_index[None, :] >= 0)
        )
        return attend_block(carry, query_heads, piece[:count, :HD], piece[:count, HD:], allowed)

    state = (
        jnp.full((count, heads), NEGATIVE, jnp.float32),
        jnp.zeros((count, heads), jnp.float32),
        jnp.zeros((count, heads, HD), jnp.float32),
    )
    for piece, number in pieces:
        state = visit(state, piece, number)
    attended = (state[2] / state[1][:, :, None]).astype(jnp.bfloat16).reshape(count, heads * HD)
    hidden_part = w_gate.shape[2]
    packed = jnp.concatenate([w_gate[0], w_up[0], w_down[0].T], axis=1)
    across = lax.ppermute(packed, "tp", [(source, source ^ 2) for source in range(tp_count)])
    attended, across = lax.optimization_barrier((attended, across))
    sibling = [(source, source ^ 1) for source in range(tp_count)]
    weight_parts = [packed, across, lax.ppermute(packed, "tp", sibling), lax.ppermute(across, "tp", sibling)]
    projected = jnp.dot(attended, w_out, preferred_element_type=jnp.float32)
    experts = lax.axis_size("seq") * w_gate.shape[0]
    choose = expert_picks.shape[1]
    capacity = count * choose * 5 // (4 * experts)
    share = capacity // tp_count
    slots = experts * share
    onehot = (expert_picks[:, :, None] == jnp.arange(experts, dtype=jnp.int32)[None, None, :]).astype(
        jnp.float32
    )
    earlier = (
        jnp.arange(count, dtype=jnp.int32)[:, None] > jnp.arange(count, dtype=jnp.int32)[None, :]
    ).astype(jnp.bfloat16)
    before = jnp.dot(
        earlier, jnp.sum(onehot, axis=1).astype(jnp.bfloat16), preferred_element_type=jnp.float32
    )
    ranks = jnp.sum(before[:, None, :] * onehot, axis=2).astype(jnp.int32)
    owner = ranks // share
    slot = expert_picks * share + ranks % share
    mine_slot = jnp.where(owner == tp_index, slot, slots)
    slot_range = jnp.arange(slots, dtype=jnp.int32)
    placing = jnp.sum(
        (mine_slot[:, :, None] == slot_range[None, None, :]).astype(jnp.bfloat16), axis=1
    ).T
    part_width = tokens.shape[1] // tp_count
    sibling_sum = lax.ppermute(projected.astype(jnp.bfloat16), "tp", sibling)
    chip_sum = projected + sibling_sum.astype(jnp.float32)
    half_width = chip_sum.shape[1] // 2
    own_half = lax.dynamic_slice_in_dim(chip_sum, core * half_width, half_width, 1)
    partner = [(lane, lane ^ 2) for lane in range(tp_count)]
    own_half = own_half + lax.ppermute(own_half.astype(jnp.bfloat16), "tp", partner).astype(jnp.float32)
    other_half = lax.ppermute(own_half.astype(jnp.bfloat16), "tp", sibling).astype(jnp.float32)
    summed = jnp.where(
        core == 0,
        jnp.concatenate([own_half, other_half], axis=1),
        jnp.concatenate([other_half, own_half], axis=1),
    )
    summed, weight_parts = lax.optimization_barrier((summed, weight_parts))
    residual = tokens.astype(jnp.float32) + summed
    mixed_in = row_norm(residual, ffn_gain).astype(jnp.bfloat16)
    columns = mixed_in.shape[1]
    rows = jnp.dot(placing, mixed_in, preferred_element_type=jnp.float32).astype(jnp.bfloat16)
    arrived = lax.all_to_all(rows, "seq", split_axis=0, concat_axis=0, tiled=True)
    gate_full = jnp.concatenate([part[:, :hidden_part] for part in weight_parts], axis=1)
    up_full = jnp.concatenate([part[:, hidden_part : 2 * hidden_part] for part in weight_parts], axis=1)
    down_full = (
        jnp.concatenate([part[:, 2 * hidden_part :] for part in weight_parts], axis=1)
        .reshape(tp_count, part_width, tp_count * hidden_part)
        .transpose(0, 2, 1)
    )
    gate_part = jnp.dot(arrived, gate_full, preferred_element_type=jnp.float32)
    up_part = jnp.dot(arrived, up_full, preferred_element_type=jnp.float32)
    hidden = (jax.nn.relu(gate_part) * up_part).astype(jnp.bfloat16)
    expert_out = jnp.einsum("rf,cfd->crd", hidden, down_full, preferred_element_type=jnp.float32)
    outgoing = expert_out.astype(jnp.bfloat16).reshape(tp_count * slots, part_width)
    mine = lax.all_to_all(outgoing, ("tp", "seq"), split_axis=0, concat_axis=0, tiled=True)
    residual_part = lax.dynamic_slice_in_dim(residual, tp_index * part_width, part_width, 1)
    every_slot = jnp.arange(experts * capacity, dtype=jnp.int32)
    picked = (owner * slots + slot)[:, :, None] == every_slot[None, None, :]
    scales = jnp.sum(jnp.where(picked, gate_weights[:, :, None], 0.0), axis=1)
    high = scales.astype(jnp.bfloat16)
    low = (scales - high.astype(jnp.float32)).astype(jnp.bfloat16)
    mixture = jnp.dot(high, mine, preferred_element_type=jnp.float32) + jnp.dot(
        low, mine, preferred_element_type=jnp.float32
    )
    layer_out = (residual_part + mixture).astype(jnp.bfloat16)
    return (layer_out, kv_pages)


def solution(mesh):
    placed = (
        P("seq", None),
        P("seq"),
        P(),
        P(None, "tp"),
        P(),
        P("tp", None),
        P(),
        P("seq", None, "tp"),
        P("seq", None, "tp"),
        P("seq", "tp", None),
        P("seq", None),
        P("seq", None),
        P("seq"),
    )
    return jax.shard_map(
        per_device,
        mesh=mesh,
        in_specs=placed,
        out_specs=(P("seq", "tp"), P("seq", None, "tp")),
        check_vma=False,
    )
```

```python
import jax
import jax.numpy as jnp
from jax import lax
from jax.sharding import PartitionSpec as P

HQ = 12
HK = 2
HD = 128


EPSILON = 1e-06
NEGATIVE = -1e30


def shifted(value, axis, steps):
    count = lax.axis_size(axis)
    leading, last = (max(0, -steps), min(count, count - steps))
    return lax.ppermute(value, axis, [(source, source + steps) for source in range(leading, last)])


def row_norm(values, gain):
    values = values.astype(jnp.float32)
    factor = lax.rsqrt(jnp.mean(values * values, axis=-1, keepdims=True) + EPSILON)
    return values * factor * gain


def attend_block(carry, queries, key_block, value_block, allowed):
    running, total, accum = carry
    scores = jnp.einsum(
        "qhd,kd->qhk", queries, key_block, preferred_element_type=jnp.float32
    ) * HD ** (-0.5)
    open_mask = allowed[:, None, :]
    highest = jnp.max(jnp.where(open_mask, scores, NEGATIVE), axis=2)
    renewed = jnp.maximum(running, highest)
    weights = jnp.where(open_mask, jnp.exp(scores - renewed[:, :, None]), 0.0)
    factor = jnp.exp(running - renewed)
    total = total * factor + jnp.sum(weights, axis=2)
    accum = accum * factor[:, :, None] + jnp.einsum(
        "qhk,kd->qhd", weights.astype(jnp.bfloat16), value_block, preferred_element_type=jnp.float32
    )
    return (renewed, total, accum)


def per_device(
    tokens,
    segment_ids,
    attn_gain,
    w_query,
    w_kv,
    w_out,
    ffn_gain,
    w_gate,
    w_up,
    w_down,
    expert_picks,
    gate_weights,
    page_table,
):
    count = tokens.shape[0]
    seq_index = lax.axis_index("seq")
    tp_index = lax.axis_index("tp")
    tp_count = lax.axis_size("tp")
    normed = row_norm(tokens, attn_gain).astype(jnp.bfloat16)
    queries = jnp.dot(normed, w_query, preferred_element_type=jnp.float32).astype(jnp.bfloat16)
    keyval = jnp.dot(normed, w_kv, preferred_element_type=jnp.float32).astype(jnp.bfloat16)
    cache_width = keyval.shape[1] // tp_count
    cache_columns = lax.dynamic_slice_in_dim(keyval, tp_index * cache_width, cache_width, 1)
    page_rows = page_table.shape[0]
    page_length = count // page_rows
    local_pages = page_table - seq_index * page_rows
    kv_pages = (
        jnp.zeros((page_rows, page_length, cache_width), jnp.bfloat16)
        .at[local_pages]
        .set(cache_columns.reshape(page_rows, page_length, cache_width))
    )
    heads = queries.shape[1] // HD
    group = tp_index * heads // (HQ // HK)
    key_head = lax.dynamic_slice_in_dim(keyval, group * HD, HD, 1)
    value_head = lax.dynamic_slice_in_dim(keyval, (HK + group) * HD, HD, 1)
    query_heads = queries.reshape(count, heads, HD)
    query_index = seq_index * count + jnp.arange(count, dtype=jnp.int32)
    width = 2 * HD
    code_rows = 2 * count // width
    code = jnp.stack([segment_ids // 256, segment_ids % 256]).astype(jnp.bfloat16).reshape(code_rows, width)
    code = jnp.concatenate([code, jnp.zeros((16 - code_rows % 16, width), jnp.bfloat16)], axis=0)
    own_piece = jnp.concatenate([jnp.concatenate([key_head, value_head], axis=1), code], axis=0)
    reach_steps = lax.axis_size("seq") // 4
    seq_count = lax.axis_size("seq")
    rounds = reach_steps // 2
    core = tp_index % 2
    fetched = []
    for number in range(1, rounds + 1):
        pairs = []
        for source_seq in range(seq_count):
            for lane in range(tp_count):
                target_seq = source_seq + number + rounds * (lane % 2)
                if target_seq < seq_count:
                    pairs.append((source_seq * tp_count + lane, target_seq * tp_count + lane))
        fetched.append(lax.ppermute(own_piece, ("seq", "tp"), pairs))
    swapped = lax.ppermute(jnp.stack(fetched), "tp", [(lane, lane ^ 1) for lane in range(tp_count)])
    fetched = jnp.stack(fetched)
    steps = jnp.arange(1, rounds + 1, dtype=jnp.int32)
    groups = [(fetched, steps + rounds * core), (swapped, steps + rounds * (1 - core))]

    def visit(carry, piece, number):
        start = (seq_index - number) * count
        key_index = start + jnp.arange(count, dtype=jnp.int32)
        coded = piece[count : count + code_rows].reshape(2, count).astype(jnp.int32)
        segment_piece = coded[0] * 256 + coded[1]
        allowed = (
            (segment_piece[None, :] == segment_ids[:, None])
            & (key_index[None, :] <= query_index[:, None])
            & (key_index[None, :] >= 0)
        )
        return attend_block(carry, query_heads, piece[:count, :HD], piece[:count, HD:], allowed)

    state = (
        jnp.full((count, heads), NEGATIVE, jnp.float32),
        jnp.zeros((count, heads), jnp.float32),
        jnp.zeros((count, heads, HD), jnp.float32),
    )
    state = visit(state, own_piece, 0)

    def step(carry, inputs):
        piece, number = inputs
        return (visit(carry, piece, number), None)

    for stacked, numbers in groups:
        state, ignored = lax.scan(step, state, (stacked, numbers))
    attended = (state[2] / state[1][:, :, None]).astype(jnp.bfloat16).reshape(count, heads * HD)
    hidden_part = w_gate.shape[2]
    packed = jnp.concatenate([w_gate[0], w_up[0], w_down[0].T], axis=1)
    across = lax.ppermute(packed, "tp", [(source, source ^ 2) for source in range(tp_count)])
    attended, across = lax.optimization_barrier((attended, across))
    sibling = [(source, source ^ 1) for source in range(tp_count)]
    weight_parts = [packed, across, lax.ppermute(packed, "tp", sibling), lax.ppermute(across, "tp", sibling)]
    projected = jnp.dot(attended, w_out, preferred_element_type=jnp.float32)
    experts = lax.axis_size("seq") * w_gate.shape[0]
    choose = expert_picks.shape[1]
    capacity = count * choose * 5 // (4 * experts)
    share = capacity // tp_count
    slots = experts * share
    onehot = (expert_picks[:, :, None] == jnp.arange(experts, dtype=jnp.int32)[None, None, :]).astype(
        jnp.float32
    )
    earlier = (
        jnp.arange(count, dtype=jnp.int32)[:, None] > jnp.arange(count, dtype=jnp.int32)[None, :]
    ).astype(jnp.bfloat16)
    before = jnp.dot(
        earlier, jnp.sum(onehot, axis=1).astype(jnp.bfloat16), preferred_element_type=jnp.float32
    )
    ranks = jnp.sum(before[:, None, :] * onehot, axis=2).astype(jnp.int32)
    owner = ranks // share
    slot = expert_picks * share + ranks % share
    mine_slot = jnp.where(owner == tp_index, slot, slots)
    slot_range = jnp.arange(slots, dtype=jnp.int32)
    placing = jnp.sum(
        (mine_slot[:, :, None] == slot_range[None, None, :]).astype(jnp.bfloat16), axis=1
    ).T
    part_width = tokens.shape[1] // tp_count
    sibling_sum = lax.ppermute(projected.astype(jnp.bfloat16), "tp", sibling)
    chip_sum = projected + sibling_sum.astype(jnp.float32)
    half_width = chip_sum.shape[1] // 2
    own_half = lax.dynamic_slice_in_dim(chip_sum, core * half_width, half_width, 1)
    partner = [(lane, lane ^ 2) for lane in range(tp_count)]
    own_half = own_half + lax.ppermute(own_half.astype(jnp.bfloat16), "tp", partner).astype(jnp.float32)
    other_half = lax.ppermute(own_half.astype(jnp.bfloat16), "tp", sibling).astype(jnp.float32)
    summed = jnp.where(
        core == 0,
        jnp.concatenate([own_half, other_half], axis=1),
        jnp.concatenate([other_half, own_half], axis=1),
    )
    summed, weight_parts = lax.optimization_barrier((summed, weight_parts))
    residual = tokens.astype(jnp.float32) + summed
    mixed_in = row_norm(residual, ffn_gain).astype(jnp.bfloat16)
    columns = mixed_in.shape[1]
    rows = jnp.dot(placing, mixed_in, preferred_element_type=jnp.float32).astype(jnp.bfloat16)
    arrived = lax.all_to_all(rows, "seq", split_axis=0, concat_axis=0, tiled=True)
    gate_full = jnp.concatenate([part[:, :hidden_part] for part in weight_parts], axis=1)
    up_full = jnp.concatenate([part[:, hidden_part : 2 * hidden_part] for part in weight_parts], axis=1)
    down_full = jnp.concatenate([part[:, 2 * hidden_part :] for part in weight_parts], axis=1).T
    gate_part = jnp.dot(arrived, gate_full, preferred_element_type=jnp.float32)
    up_part = jnp.dot(arrived, up_full, preferred_element_type=jnp.float32)
    hidden = (jax.nn.relu(gate_part) * up_part).astype(jnp.bfloat16)
    expert_out = jnp.dot(hidden, down_full, preferred_element_type=jnp.float32).astype(jnp.bfloat16)
    sources = lax.axis_size("seq")
    outgoing = (
        expert_out.reshape(sources, share, tp_count, part_width)
        .transpose(0, 2, 1, 3)
        .reshape(sources * tp_count * share, part_width)
    )
    mine = lax.all_to_all(outgoing, ("seq", "tp"), split_axis=0, concat_axis=0, tiled=True)
    residual_part = lax.dynamic_slice_in_dim(residual, tp_index * part_width, part_width, 1)
    every_slot = jnp.arange(experts * capacity, dtype=jnp.int32)
    picked = (expert_picks * capacity + ranks)[:, :, None] == every_slot[None, None, :]
    scales = jnp.sum(jnp.where(picked, gate_weights[:, :, None], 0.0), axis=1)
    high = scales.astype(jnp.bfloat16)
    low = (scales - high.astype(jnp.float32)).astype(jnp.bfloat16)
    mixture = jnp.dot(high, mine, preferred_element_type=jnp.float32) + jnp.dot(
        low, mine, preferred_element_type=jnp.float32
    )
    layer_out = (residual_part + mixture).astype(jnp.bfloat16)
    return (layer_out, kv_pages)


def solution(mesh):
    placed = (
        P("seq", None),
        P("seq"),
        P(),
        P(None, "tp"),
        P(),
        P("tp", None),
        P(),
        P("seq", None, "tp"),
        P("seq", None, "tp"),
        P("seq", "tp", None),
        P("seq", None),
        P("seq", None),
        P("seq"),
    )
    return jax.shard_map(
        per_device,
        mesh=mesh,
        in_specs=placed,
        out_specs=(P("seq", "tp"), P("seq", None, "tp")),
        check_vma=False,
    )
```

```python
import jax
import jax.numpy as jnp
from jax import lax
from jax.sharding import PartitionSpec as P

HQ = 12
HK = 2
HD = 128


EPSILON = 1e-06
NEGATIVE = -1e30


def shifted(value, axis, steps):
    count = lax.axis_size(axis)
    leading, last = (max(0, -steps), min(count, count - steps))
    return lax.ppermute(value, axis, [(source, source + steps) for source in range(leading, last)])


def row_norm(values, gain):
    values = values.astype(jnp.float32)
    factor = lax.rsqrt(jnp.mean(values * values, axis=-1, keepdims=True) + EPSILON)
    return values * factor * gain


def attend_block(carry, queries, key_block, value_block, allowed):
    running, total, accum = carry
    scores = jnp.einsum(
        "qhd,kd->qhk", queries, key_block, preferred_element_type=jnp.float32
    ) * HD ** (-0.5)
    open_mask = allowed[:, None, :]
    highest = jnp.max(jnp.where(open_mask, scores, NEGATIVE), axis=2)
    renewed = jnp.maximum(running, highest)
    weights = jnp.where(open_mask, jnp.exp(scores - renewed[:, :, None]), 0.0)
    factor = jnp.exp(running - renewed)
    total = total * factor + jnp.sum(weights, axis=2)
    accum = accum * factor[:, :, None] + jnp.einsum(
        "qhk,kd->qhd", weights.astype(jnp.bfloat16), value_block, preferred_element_type=jnp.float32
    )
    return (renewed, total, accum)


def per_device(
    tokens,
    segment_ids,
    attn_gain,
    w_query,
    w_kv,
    w_out,
    ffn_gain,
    w_gate,
    w_up,
    w_down,
    expert_picks,
    gate_weights,
    page_table,
):
    count = tokens.shape[0]
    seq_index = lax.axis_index("seq")
    tp_index = lax.axis_index("tp")
    tp_count = lax.axis_size("tp")
    normed = row_norm(tokens, attn_gain).astype(jnp.bfloat16)
    queries = jnp.dot(normed, w_query, preferred_element_type=jnp.float32).astype(jnp.bfloat16)
    keyval = jnp.dot(normed, w_kv, preferred_element_type=jnp.float32).astype(jnp.bfloat16)
    cache_width = keyval.shape[1] // tp_count
    cache_columns = lax.dynamic_slice_in_dim(keyval, tp_index * cache_width, cache_width, 1)
    page_rows = page_table.shape[0]
    page_length = count // page_rows
    local_pages = page_table - seq_index * page_rows
    kv_pages = (
        jnp.zeros((page_rows, page_length, cache_width), jnp.bfloat16)
        .at[local_pages]
        .set(cache_columns.reshape(page_rows, page_length, cache_width))
    )
    heads = queries.shape[1] // HD
    group = tp_index * heads // (HQ // HK)
    key_head = lax.dynamic_slice_in_dim(keyval, group * HD, HD, 1)
    value_head = lax.dynamic_slice_in_dim(keyval, (HK + group) * HD, HD, 1)
    query_heads = queries.reshape(count, heads, HD)
    query_index = seq_index * count + jnp.arange(count, dtype=jnp.int32)
    width = 2 * HD
    code_rows = 2 * count // width
    code = jnp.stack([segment_ids // 256, segment_ids % 256]).astype(jnp.bfloat16).reshape(code_rows, width)
    code = jnp.concatenate([code, jnp.zeros((16 - code_rows % 16, width), jnp.bfloat16)], axis=0)
    own_piece = jnp.concatenate([jnp.concatenate([key_head, value_head], axis=1), code], axis=0)
    reach_steps = lax.axis_size("seq") // 4
    seq_count = lax.axis_size("seq")
    rounds = reach_steps // 2
    core = tp_index % 2
    fetched = []
    for number in range(1, rounds + 1):
        pairs = []
        for source_seq in range(seq_count):
            for lane in range(tp_count):
                target_seq = source_seq + number + rounds * (lane % 2)
                if target_seq < seq_count:
                    pairs.append((source_seq * tp_count + lane, target_seq * tp_count + lane))
        fetched.append(lax.ppermute(own_piece, ("seq", "tp"), pairs))
    swapped = lax.ppermute(jnp.stack(fetched), "tp", [(lane, lane ^ 1) for lane in range(tp_count)])
    pieces = [(own_piece, 0)]
    pieces += [(piece, number + 1 + rounds * core) for number, piece in enumerate(fetched)]
    pieces += [(swapped[number], number + 1 + rounds * (1 - core)) for number in range(rounds)]

    def visit(carry, piece, number):
        start = (seq_index - number) * count
        key_index = start + jnp.arange(count, dtype=jnp.int32)
        coded = piece[count : count + code_rows].reshape(2, count).astype(jnp.int32)
        segment_piece = coded[0] * 256 + coded[1]
        allowed = (
            (segment_piece[None, :] == segment_ids[:, None])
            & (key_index[None, :] <= query_index[:, None])
            & (key_index[None, :] >= 0)
        )
        return attend_block(carry, query_heads, piece[:count, :HD], piece[:count, HD:], allowed)

    state = (
        jnp.full((count, heads), NEGATIVE, jnp.float32),
        jnp.zeros((count, heads), jnp.float32),
        jnp.zeros((count, heads, HD), jnp.float32),
    )
    for piece, number in pieces:
        state = visit(state, piece, number)
    attended = (state[2] / state[1][:, :, None]).astype(jnp.bfloat16).reshape(count, heads * HD)
    hidden_part = w_gate.shape[2]
    packed = jnp.concatenate([w_gate[0], w_up[0], w_down[0].T], axis=1)
    across = lax.ppermute(packed, "tp", [(source, source ^ 2) for source in range(tp_count)])
    attended, across = lax.optimization_barrier((attended, across))
    sibling = [(source, source ^ 1) for source in range(tp_count)]
    weight_parts = [packed, across, lax.ppermute(packed, "tp", sibling), lax.ppermute(across, "tp", sibling)]
    projected = jnp.dot(attended, w_out, preferred_element_type=jnp.float32)
    experts = lax.axis_size("seq") * w_gate.shape[0]
    choose = expert_picks.shape[1]
    capacity = count * choose * 5 // (4 * experts)
    share = capacity // tp_count
    slots = experts * share
    onehot = (expert_picks[:, :, None] == jnp.arange(experts, dtype=jnp.int32)[None, None, :]).astype(
        jnp.float32
    )
    earlier = (
        jnp.arange(count, dtype=jnp.int32)[:, None] > jnp.arange(count, dtype=jnp.int32)[None, :]
    ).astype(jnp.bfloat16)
    before = jnp.dot(
        earlier, jnp.sum(onehot, axis=1).astype(jnp.bfloat16), preferred_element_type=jnp.float32
    )
    ranks = jnp.sum(before[:, None, :] * onehot, axis=2).astype(jnp.int32)
    owner = ranks // share
    slot = expert_picks * share + ranks % share
    mine_slot = jnp.where(owner == tp_index, slot, slots)
    slot_range = jnp.arange(slots, dtype=jnp.int32)
    placing = jnp.sum(
        (mine_slot[:, :, None] == slot_range[None, None, :]).astype(jnp.bfloat16), axis=1
    ).T
    part_width = tokens.shape[1] // tp_count
    sibling_sum = lax.ppermute(projected.astype(jnp.bfloat16), "tp", sibling)
    chip_sum = projected + sibling_sum.astype(jnp.float32)
    half_width = chip_sum.shape[1] // 2
    own_half = lax.dynamic_slice_in_dim(chip_sum, core * half_width, half_width, 1)
    partner = [(lane, lane ^ 2) for lane in range(tp_count)]
    own_half = own_half + lax.ppermute(own_half.astype(jnp.bfloat16), "tp", partner).astype(jnp.float32)
    other_half = lax.ppermute(own_half.astype(jnp.bfloat16), "tp", sibling).astype(jnp.float32)
    summed = jnp.where(
        core == 0,
        jnp.concatenate([own_half, other_half], axis=1),
        jnp.concatenate([other_half, own_half], axis=1),
    )
    summed, weight_parts = lax.optimization_barrier((summed, weight_parts))
    residual = tokens.astype(jnp.float32) + summed
    mixed_in = row_norm(residual, ffn_gain).astype(jnp.bfloat16)
    columns = mixed_in.shape[1]
    rows = jnp.dot(placing, mixed_in, preferred_element_type=jnp.float32).astype(jnp.bfloat16)
    rows = rows.reshape(experts, share, columns)
    pieces_of = 2
    piece_slots = share // pieces_of
    sent = [
        lax.all_to_all(
            rows[:, number * piece_slots : (number + 1) * piece_slots].reshape(experts * piece_slots, columns),
            "seq", split_axis=0, concat_axis=0, tiled=True,
        )
        for number in range(pieces_of)
    ]
    sent[0], weight_parts = lax.optimization_barrier((sent[0], weight_parts))
    gate_full = jnp.concatenate([part[:, :hidden_part] for part in weight_parts], axis=1)
    up_full = jnp.concatenate([part[:, hidden_part : 2 * hidden_part] for part in weight_parts], axis=1)
    down_full = jnp.concatenate([part[:, 2 * hidden_part :] for part in weight_parts], axis=1).T
    sources = lax.axis_size("seq")
    received = []
    for arrived in sent:
        gate_part = jnp.dot(arrived, gate_full, preferred_element_type=jnp.float32)
        up_part = jnp.dot(arrived, up_full, preferred_element_type=jnp.float32)
        hidden = (jax.nn.relu(gate_part) * up_part).astype(jnp.bfloat16)
        expert_out = jnp.dot(hidden, down_full, preferred_element_type=jnp.float32).astype(jnp.bfloat16)
        outgoing = (
            expert_out.reshape(sources, piece_slots, tp_count, part_width)
            .transpose(0, 2, 1, 3)
            .reshape(sources * tp_count * piece_slots, part_width)
        )
        received.append(lax.all_to_all(outgoing, ("seq", "tp"), split_axis=0, concat_axis=0, tiled=True))
    mine = jnp.concatenate(received, axis=0)
    residual_part = lax.dynamic_slice_in_dim(residual, tp_index * part_width, part_width, 1)
    every_slot = jnp.arange(experts * capacity, dtype=jnp.int32)
    within = ranks % share
    flat = (within // piece_slots) * (experts * capacity // pieces_of) + (
        (expert_picks * tp_count + owner) * piece_slots + within % piece_slots
    )
    picked = flat[:, :, None] == every_slot[None, None, :]
    scales = jnp.sum(jnp.where(picked, gate_weights[:, :, None], 0.0), axis=1)
    high = scales.astype(jnp.bfloat16)
    low = (scales - high.astype(jnp.float32)).astype(jnp.bfloat16)
    mixture = jnp.dot(high, mine, preferred_element_type=jnp.float32) + jnp.dot(
        low, mine, preferred_element_type=jnp.float32
    )
    layer_out = (residual_part + mixture).astype(jnp.bfloat16)
    return (layer_out, kv_pages)


def solution(mesh):
    placed = (
        P("seq", None),
        P("seq"),
        P(),
        P(None, "tp"),
        P(),
        P("tp", None),
        P(),
        P("seq", None, "tp"),
        P("seq", None, "tp"),
        P("seq", "tp", None),
        P("seq", None),
        P("seq", None),
        P("seq"),
    )
    return jax.shard_map(
        per_device,
        mesh=mesh,
        in_specs=placed,
        out_specs=(P("seq", "tp"), P("seq", None, "tp")),
        check_vma=False,
    )
```

```python
import jax
import jax.numpy as jnp
from jax import lax
from jax.sharding import PartitionSpec as P

HQ = 12
HK = 2
HD = 128


EPSILON = 1e-06
NEGATIVE = -1e30


def shifted(value, axis, steps):
    count = lax.axis_size(axis)
    leading, last = (max(0, -steps), min(count, count - steps))
    return lax.ppermute(value, axis, [(source, source + steps) for source in range(leading, last)])


def row_norm(values, gain):
    values = values.astype(jnp.float32)
    factor = lax.rsqrt(jnp.mean(values * values, axis=-1, keepdims=True) + EPSILON)
    return values * factor * gain


def attend_block(carry, queries, key_block, value_block, allowed):
    running, total, accum = carry
    scores = jnp.einsum(
        "qhd,kd->qhk", queries, key_block, preferred_element_type=jnp.float32
    ) * HD ** (-0.5)
    open_mask = allowed[:, None, :]
    highest = jnp.max(jnp.where(open_mask, scores, NEGATIVE), axis=2)
    renewed = jnp.maximum(running, highest)
    weights = jnp.where(open_mask, jnp.exp(scores - renewed[:, :, None]), 0.0)
    factor = jnp.exp(running - renewed)
    total = total * factor + jnp.sum(weights, axis=2)
    accum = accum * factor[:, :, None] + jnp.einsum(
        "qhk,kd->qhd", weights.astype(jnp.bfloat16), value_block, preferred_element_type=jnp.float32
    )
    return (renewed, total, accum)


def per_device(
    tokens,
    segment_ids,
    attn_gain,
    w_query,
    w_kv,
    w_out,
    ffn_gain,
    w_gate,
    w_up,
    w_down,
    expert_picks,
    gate_weights,
    page_table,
):
    count = tokens.shape[0]
    seq_index = lax.axis_index("seq")
    tp_index = lax.axis_index("tp")
    tp_count = lax.axis_size("tp")
    normed = row_norm(tokens, attn_gain).astype(jnp.bfloat16)
    queries = jnp.dot(normed, w_query, preferred_element_type=jnp.float32).astype(jnp.bfloat16)
    keyval = jnp.dot(normed, w_kv, preferred_element_type=jnp.float32).astype(jnp.bfloat16)
    cache_width = keyval.shape[1] // tp_count
    cache_columns = lax.dynamic_slice_in_dim(keyval, tp_index * cache_width, cache_width, 1)
    page_rows = page_table.shape[0]
    page_length = count // page_rows
    local_pages = page_table - seq_index * page_rows
    kv_pages = (
        jnp.zeros((page_rows, page_length, cache_width), jnp.bfloat16)
        .at[local_pages]
        .set(cache_columns.reshape(page_rows, page_length, cache_width))
    )
    heads = queries.shape[1] // HD
    group = tp_index * heads // (HQ // HK)
    key_head = lax.dynamic_slice_in_dim(keyval, group * HD, HD, 1)
    value_head = lax.dynamic_slice_in_dim(keyval, (HK + group) * HD, HD, 1)
    query_heads = queries.reshape(count, heads, HD)
    query_index = seq_index * count + jnp.arange(count, dtype=jnp.int32)
    width = 2 * HD
    code_rows = 2 * count // width
    code = jnp.stack([segment_ids // 256, segment_ids % 256]).astype(jnp.bfloat16).reshape(code_rows, width)
    code = jnp.concatenate([code, jnp.zeros((16 - code_rows % 16, width), jnp.bfloat16)], axis=0)
    own_piece = jnp.concatenate([jnp.concatenate([key_head, value_head], axis=1), code], axis=0)
    reach_steps = lax.axis_size("seq") // 4
    seq_count = lax.axis_size("seq")
    rounds = reach_steps // 2
    core = tp_index % 2
    fetched = []
    for number in range(1, rounds + 1):
        pairs = []
        for source_seq in range(seq_count):
            for lane in range(tp_count):
                target_seq = source_seq + number + rounds * (lane % 2)
                if target_seq < seq_count:
                    pairs.append((source_seq * tp_count + lane, target_seq * tp_count + lane))
        fetched.append(lax.ppermute(own_piece, ("seq", "tp"), pairs))
    swapped = lax.ppermute(jnp.stack(fetched), "tp", [(lane, lane ^ 1) for lane in range(tp_count)])
    pieces = [(own_piece, 0)]
    pieces += [(piece, number + 1 + rounds * core) for number, piece in enumerate(fetched)]
    pieces += [(swapped[number], number + 1 + rounds * (1 - core)) for number in range(rounds)]

    def visit(carry, group_pieces):
        key_parts, value_parts, segment_parts, index_parts = [], [], [], []
        for piece, number in group_pieces:
            start = (seq_index - number) * count
            index_parts.append(start + jnp.arange(count, dtype=jnp.int32))
            coded = piece[count : count + code_rows].reshape(2, count).astype(jnp.int32)
            segment_parts.append(coded[0] * 256 + coded[1])
            key_parts.append(piece[:count, :HD])
            value_parts.append(piece[:count, HD:])
        key_index = jnp.concatenate(index_parts)
        segment_piece = jnp.concatenate(segment_parts)
        allowed = (
            (segment_piece[None, :] == segment_ids[:, None])
            & (key_index[None, :] <= query_index[:, None])
            & (key_index[None, :] >= 0)
        )
        keys = jnp.concatenate(key_parts, axis=0)
        values = jnp.concatenate(value_parts, axis=0)
        return attend_block(carry, query_heads, keys, values, allowed)

    state = (
        jnp.full((count, heads), NEGATIVE, jnp.float32),
        jnp.zeros((count, heads), jnp.float32),
        jnp.zeros((count, heads, HD), jnp.float32),
    )
    state = visit(state, pieces[:1])
    for first in range(1, len(pieces), 2):
        state = visit(state, pieces[first : first + 2])
    attended = (state[2] / state[1][:, :, None]).astype(jnp.bfloat16).reshape(count, heads * HD)
    hidden_part = w_gate.shape[2]
    packed = jnp.concatenate([w_gate[0], w_up[0], w_down[0].T], axis=1)
    across = lax.ppermute(packed, "tp", [(source, source ^ 2) for source in range(tp_count)])
    attended, across = lax.optimization_barrier((attended, across))
    sibling = [(source, source ^ 1) for source in range(tp_count)]
    weight_parts = [packed, across, lax.ppermute(packed, "tp", sibling), lax.ppermute(across, "tp", sibling)]
    projected = jnp.dot(attended, w_out, preferred_element_type=jnp.float32)
    experts = lax.axis_size("seq") * w_gate.shape[0]
    choose = expert_picks.shape[1]
    capacity = count * choose * 5 // (4 * experts)
    share = capacity // tp_count
    slots = experts * share
    onehot = (expert_picks[:, :, None] == jnp.arange(experts, dtype=jnp.int32)[None, None, :]).astype(
        jnp.float32
    )
    earlier = (
        jnp.arange(count, dtype=jnp.int32)[:, None] > jnp.arange(count, dtype=jnp.int32)[None, :]
    ).astype(jnp.bfloat16)
    before = jnp.dot(
        earlier, jnp.sum(onehot, axis=1).astype(jnp.bfloat16), preferred_element_type=jnp.float32
    )
    ranks = jnp.sum(before[:, None, :] * onehot, axis=2).astype(jnp.int32)
    owner = ranks // share
    slot = expert_picks * share + ranks % share
    mine_slot = jnp.where(owner == tp_index, slot, slots)
    slot_range = jnp.arange(slots, dtype=jnp.int32)
    placing = jnp.sum(
        (mine_slot[:, :, None] == slot_range[None, None, :]).astype(jnp.bfloat16), axis=1
    ).T
    part_width = tokens.shape[1] // tp_count
    sibling_sum = lax.ppermute(projected.astype(jnp.bfloat16), "tp", sibling)
    chip_sum = projected + sibling_sum.astype(jnp.float32)
    half_width = chip_sum.shape[1] // 2
    own_half = lax.dynamic_slice_in_dim(chip_sum, core * half_width, half_width, 1)
    partner = [(lane, lane ^ 2) for lane in range(tp_count)]
    own_half = own_half + lax.ppermute(own_half.astype(jnp.bfloat16), "tp", partner).astype(jnp.float32)
    other_half = lax.ppermute(own_half.astype(jnp.bfloat16), "tp", sibling).astype(jnp.float32)
    summed = jnp.where(
        core == 0,
        jnp.concatenate([own_half, other_half], axis=1),
        jnp.concatenate([other_half, own_half], axis=1),
    )
    summed, weight_parts = lax.optimization_barrier((summed, weight_parts))
    residual = tokens.astype(jnp.float32) + summed
    mixed_in = row_norm(residual, ffn_gain).astype(jnp.bfloat16)
    columns = mixed_in.shape[1]
    rows = jnp.dot(placing, mixed_in, preferred_element_type=jnp.float32).astype(jnp.bfloat16)
    arrived = lax.all_to_all(rows, "seq", split_axis=0, concat_axis=0, tiled=True)
    gate_full = jnp.concatenate([part[:, :hidden_part] for part in weight_parts], axis=1)
    up_full = jnp.concatenate([part[:, hidden_part : 2 * hidden_part] for part in weight_parts], axis=1)
    down_full = jnp.concatenate([part[:, 2 * hidden_part :] for part in weight_parts], axis=1).T
    gate_part = jnp.dot(arrived, gate_full, preferred_element_type=jnp.float32)
    up_part = jnp.dot(arrived, up_full, preferred_element_type=jnp.float32)
    hidden = (jax.nn.relu(gate_part) * up_part).astype(jnp.bfloat16)
    expert_out = jnp.dot(hidden, down_full, preferred_element_type=jnp.float32).astype(jnp.bfloat16)
    sources = lax.axis_size("seq")
    outgoing = (
        expert_out.reshape(sources, share, tp_count, part_width)
        .transpose(0, 2, 1, 3)
        .reshape(sources * tp_count * share, part_width)
    )
    mine = lax.all_to_all(outgoing, ("seq", "tp"), split_axis=0, concat_axis=0, tiled=True)
    residual_part = lax.dynamic_slice_in_dim(residual, tp_index * part_width, part_width, 1)
    every_slot = jnp.arange(experts * capacity, dtype=jnp.int32)
    picked = (expert_picks * capacity + ranks)[:, :, None] == every_slot[None, None, :]
    scales = jnp.sum(jnp.where(picked, gate_weights[:, :, None], 0.0), axis=1)
    high = scales.astype(jnp.bfloat16)
    low = (scales - high.astype(jnp.float32)).astype(jnp.bfloat16)
    mixture = jnp.dot(high, mine, preferred_element_type=jnp.float32) + jnp.dot(
        low, mine, preferred_element_type=jnp.float32
    )
    layer_out = (residual_part + mixture).astype(jnp.bfloat16)
    return (layer_out, kv_pages)


def solution(mesh):
    placed = (
        P("seq", None),
        P("seq"),
        P(),
        P(None, "tp"),
        P(),
        P("tp", None),
        P(),
        P("seq", None, "tp"),
        P("seq", None, "tp"),
        P("seq", "tp", None),
        P("seq", None),
        P("seq", None),
        P("seq"),
    )
    return jax.shard_map(
        per_device,
        mesh=mesh,
        in_specs=placed,
        out_specs=(P("seq", "tp"), P("seq", None, "tp")),
        check_vma=False,
    )
```

```python
import jax
import jax.numpy as jnp
from jax import lax
from jax.sharding import PartitionSpec as P

HQ = 12
HK = 2
HD = 128


EPSILON = 1e-06
NEGATIVE = -1e30


def shifted(value, axis, steps):
    count = lax.axis_size(axis)
    leading, last = (max(0, -steps), min(count, count - steps))
    return lax.ppermute(value, axis, [(source, source + steps) for source in range(leading, last)])


def row_norm(values, gain):
    values = values.astype(jnp.float32)
    factor = lax.rsqrt(jnp.mean(values * values, axis=-1, keepdims=True) + EPSILON)
    return values * factor * gain


def attend_block(carry, queries, key_block, value_block, allowed):
    running, total, accum = carry
    scores = jnp.einsum(
        "qhd,kd->qhk", queries, key_block, preferred_element_type=jnp.float32
    ) * HD ** (-0.5)
    open_mask = allowed[:, None, :]
    highest = jnp.max(jnp.where(open_mask, scores, NEGATIVE), axis=2)
    renewed = jnp.maximum(running, highest)
    weights = jnp.where(open_mask, jnp.exp(scores - renewed[:, :, None]), 0.0)
    factor = jnp.exp(running - renewed)
    total = total * factor + jnp.sum(weights, axis=2)
    accum = accum * factor[:, :, None] + jnp.einsum(
        "qhk,kd->qhd", weights.astype(jnp.bfloat16), value_block, preferred_element_type=jnp.float32
    )
    return (renewed, total, accum)


def per_device(
    tokens,
    segment_ids,
    attn_gain,
    w_query,
    w_kv,
    w_out,
    ffn_gain,
    w_gate,
    w_up,
    w_down,
    expert_picks,
    gate_weights,
    page_table,
):
    count = tokens.shape[0]
    seq_index = lax.axis_index("seq")
    tp_index = lax.axis_index("tp")
    tp_count = lax.axis_size("tp")
    normed = row_norm(tokens, attn_gain).astype(jnp.bfloat16)
    queries = jnp.dot(normed, w_query, preferred_element_type=jnp.float32).astype(jnp.bfloat16)
    keyval = jnp.dot(normed, w_kv, preferred_element_type=jnp.float32).astype(jnp.bfloat16)
    cache_width = keyval.shape[1] // tp_count
    cache_columns = lax.dynamic_slice_in_dim(keyval, tp_index * cache_width, cache_width, 1)
    page_rows = page_table.shape[0]
    page_length = count // page_rows
    local_pages = page_table - seq_index * page_rows
    kv_pages = (
        jnp.zeros((page_rows, page_length, cache_width), jnp.bfloat16)
        .at[local_pages]
        .set(cache_columns.reshape(page_rows, page_length, cache_width))
    )
    heads = queries.shape[1] // HD
    group = tp_index * heads // (HQ // HK)
    key_head = lax.dynamic_slice_in_dim(keyval, group * HD, HD, 1)
    value_head = lax.dynamic_slice_in_dim(keyval, (HK + group) * HD, HD, 1)
    query_heads = queries.reshape(count, heads, HD)
    query_index = seq_index * count + jnp.arange(count, dtype=jnp.int32)
    width = 2 * HD
    code_rows = 2 * count // width
    code = jnp.stack([segment_ids // 256, segment_ids % 256]).astype(jnp.bfloat16).reshape(code_rows, width)
    code = jnp.concatenate([code, jnp.zeros((16 - code_rows % 16, width), jnp.bfloat16)], axis=0)
    own_piece = jnp.concatenate([jnp.concatenate([key_head, value_head], axis=1), code], axis=0)
    reach_steps = lax.axis_size("seq") // 4
    seq_count = lax.axis_size("seq")
    rounds = reach_steps // 2
    core = tp_index % 2
    fetched = []
    for number in range(1, rounds + 1):
        pairs = []
        for source_seq in range(seq_count):
            for lane in range(tp_count):
                target_seq = source_seq + number + rounds * (lane % 2)
                if target_seq < seq_count:
                    pairs.append((source_seq * tp_count + lane, target_seq * tp_count + lane))
        fetched.append(lax.ppermute(own_piece, ("seq", "tp"), pairs))
    swapped = lax.ppermute(jnp.stack(fetched), "tp", [(lane, lane ^ 1) for lane in range(tp_count)])
    pieces = [(own_piece, 0)]
    pieces += [(piece, number + 1 + rounds * core) for number, piece in enumerate(fetched)]
    pieces += [(swapped[number], number + 1 + rounds * (1 - core)) for number in range(rounds)]

    def visit(carry, piece, number):
        start = (seq_index - number) * count
        key_index = start + jnp.arange(count, dtype=jnp.int32)
        coded = piece[count : count + code_rows].reshape(2, count).astype(jnp.int32)
        segment_piece = coded[0] * 256 + coded[1]
        allowed = (
            (segment_piece[None, :] == segment_ids[:, None])
            & (key_index[None, :] <= query_index[:, None])
            & (key_index[None, :] >= 0)
        )
        return attend_block(carry, query_heads, piece[:count, :HD], piece[:count, HD:], allowed)

    state = (
        jnp.full((count, heads), NEGATIVE, jnp.float32),
        jnp.zeros((count, heads), jnp.float32),
        jnp.zeros((count, heads, HD), jnp.float32),
    )
    for piece, number in pieces:
        state = visit(state, piece, number)
    attended = (state[2] / state[1][:, :, None]).astype(jnp.bfloat16).reshape(count, heads * HD)
    hidden_part = w_gate.shape[2]
    packed = jnp.concatenate([w_gate[0], w_up[0], w_down[0].T], axis=1)
    across = lax.ppermute(packed, "tp", [(source, source ^ 2) for source in range(tp_count)])
    attended, across = lax.optimization_barrier((attended, across))
    sibling = [(source, source ^ 1) for source in range(tp_count)]
    weight_parts = [packed, across, lax.ppermute(packed, "tp", sibling), lax.ppermute(across, "tp", sibling)]
    projected = jnp.dot(attended, w_out, preferred_element_type=jnp.float32)
    experts = lax.axis_size("seq") * w_gate.shape[0]
    choose = expert_picks.shape[1]
    capacity = count * choose * 5 // (4 * experts)
    share = capacity // tp_count
    slots = experts * share
    onehot = (expert_picks[:, :, None] == jnp.arange(experts, dtype=jnp.int32)[None, None, :]).astype(
        jnp.float32
    )
    earlier = (
        jnp.arange(count, dtype=jnp.int32)[:, None] > jnp.arange(count, dtype=jnp.int32)[None, :]
    ).astype(jnp.bfloat16)
    before = jnp.dot(
        earlier, jnp.sum(onehot, axis=1).astype(jnp.bfloat16), preferred_element_type=jnp.float32
    )
    ranks = jnp.sum(before[:, None, :] * onehot, axis=2).astype(jnp.int32)
    owner = ranks // share
    slot = expert_picks * share + ranks % share
    mine_slot = jnp.where(owner == tp_index, slot, slots)
    slot_range = jnp.arange(slots, dtype=jnp.int32)
    placing = jnp.sum(
        (mine_slot[:, :, None] == slot_range[None, None, :]).astype(jnp.bfloat16), axis=1
    ).T
    part_width = tokens.shape[1] // tp_count
    sibling_sum = lax.ppermute(projected.astype(jnp.bfloat16), "tp", sibling)
    chip_sum = projected + sibling_sum.astype(jnp.float32)
    half_width = chip_sum.shape[1] // 2
    own_half = lax.dynamic_slice_in_dim(chip_sum, core * half_width, half_width, 1)
    partner = [(lane, lane ^ 2) for lane in range(tp_count)]
    own_half = own_half + lax.ppermute(own_half.astype(jnp.bfloat16), "tp", partner).astype(jnp.float32)
    other_half = lax.ppermute(own_half.astype(jnp.bfloat16), "tp", sibling).astype(jnp.float32)
    first = core == 0
    summed = jnp.concatenate(
        [jnp.where(first, own_half, other_half), jnp.where(first, other_half, own_half)], axis=1
    )
    summed, weight_parts = lax.optimization_barrier((summed, weight_parts))
    residual = tokens.astype(jnp.float32) + summed
    mixed_in = row_norm(residual, ffn_gain).astype(jnp.bfloat16)
    columns = mixed_in.shape[1]
    rows = jnp.dot(placing, mixed_in, preferred_element_type=jnp.float32).astype(jnp.bfloat16)
    arrived = lax.all_to_all(rows, "seq", split_axis=0, concat_axis=0, tiled=True)
    gate_full = jnp.concatenate([part[:, :hidden_part] for part in weight_parts], axis=1)
    up_full = jnp.concatenate([part[:, hidden_part : 2 * hidden_part] for part in weight_parts], axis=1)
    down_full = jnp.concatenate([part[:, 2 * hidden_part :] for part in weight_parts], axis=1).T
    gate_part = jnp.dot(arrived, gate_full, preferred_element_type=jnp.float32)
    up_part = jnp.dot(arrived, up_full, preferred_element_type=jnp.float32)
    hidden = (jax.nn.relu(gate_part) * up_part).astype(jnp.bfloat16)
    expert_out = jnp.dot(hidden, down_full, preferred_element_type=jnp.float32).astype(jnp.bfloat16)
    sources = lax.axis_size("seq")
    outgoing = (
        expert_out.reshape(sources, share, tp_count, part_width)
        .transpose(0, 2, 1, 3)
        .reshape(sources * tp_count * share, part_width)
    )
    mine = lax.all_to_all(outgoing, ("seq", "tp"), split_axis=0, concat_axis=0, tiled=True)
    residual_part = lax.dynamic_slice_in_dim(residual, tp_index * part_width, part_width, 1)
    every_slot = jnp.arange(experts * capacity, dtype=jnp.int32)
    picked = (expert_picks * capacity + ranks)[:, :, None] == every_slot[None, None, :]
    scales = jnp.sum(jnp.where(picked, gate_weights[:, :, None], 0.0), axis=1)
    high = scales.astype(jnp.bfloat16)
    low = (scales - high.astype(jnp.float32)).astype(jnp.bfloat16)
    both = jnp.dot(jnp.concatenate([high, low], axis=0), mine, preferred_element_type=jnp.float32)
    mixture = both[:count] + both[count:]
    layer_out = (residual_part + mixture).astype(jnp.bfloat16)
    return (layer_out, kv_pages)


def solution(mesh):
    placed = (
        P("seq", None),
        P("seq"),
        P(),
        P(None, "tp"),
        P(),
        P("tp", None),
        P(),
        P("seq", None, "tp"),
        P("seq", None, "tp"),
        P("seq", "tp", None),
        P("seq", None),
        P("seq", None),
        P("seq"),
    )
    return jax.shard_map(
        per_device,
        mesh=mesh,
        in_specs=placed,
        out_specs=(P("seq", "tp"), P("seq", None, "tp")),
        check_vma=False,
    )
```

```python
import jax
import jax.numpy as jnp
from jax import lax
from jax.sharding import PartitionSpec as P

HQ = 12
HK = 2
HD = 128


EPSILON = 1e-06
NEGATIVE = -1e30


def shifted(value, axis, steps):
    count = lax.axis_size(axis)
    leading, last = (max(0, -steps), min(count, count - steps))
    return lax.ppermute(value, axis, [(source, source + steps) for source in range(leading, last)])


def row_norm(values, gain):
    values = values.astype(jnp.float32)
    factor = lax.rsqrt(jnp.mean(values * values, axis=-1, keepdims=True) + EPSILON)
    return values * factor * gain


def attend_block(carry, queries, key_block, value_block, allowed):
    running, total, accum = carry
    scores = jnp.einsum(
        "qhd,kd->qhk", queries, key_block, preferred_element_type=jnp.float32
    ) * HD ** (-0.5)
    open_mask = allowed[:, None, :]
    highest = jnp.max(jnp.where(open_mask, scores, NEGATIVE), axis=2)
    renewed = jnp.maximum(running, highest)
    weights = jnp.where(open_mask, jnp.exp(scores - renewed[:, :, None]), 0.0)
    factor = jnp.exp(running - renewed)
    total = total * factor + jnp.sum(weights, axis=2)
    accum = accum * factor[:, :, None] + jnp.einsum(
        "qhk,kd->qhd", weights.astype(jnp.bfloat16), value_block, preferred_element_type=jnp.float32
    )
    return (renewed, total, accum)


def per_device(
    tokens,
    segment_ids,
    attn_gain,
    w_query,
    w_kv,
    w_out,
    ffn_gain,
    w_gate,
    w_up,
    w_down,
    expert_picks,
    gate_weights,
    page_table,
):
    count = tokens.shape[0]
    seq_index = lax.axis_index("seq")
    tp_index = lax.axis_index("tp")
    tp_count = lax.axis_size("tp")
    normed = row_norm(tokens, attn_gain).astype(jnp.bfloat16)
    queries = jnp.dot(normed, w_query, preferred_element_type=jnp.float32).astype(jnp.bfloat16)
    keyval = jnp.dot(normed, w_kv, preferred_element_type=jnp.float32).astype(jnp.bfloat16)
    cache_width = keyval.shape[1] // tp_count
    cache_columns = lax.dynamic_slice_in_dim(keyval, tp_index * cache_width, cache_width, 1)
    page_rows = page_table.shape[0]
    page_length = count // page_rows
    local_pages = page_table - seq_index * page_rows
    kv_pages = (
        jnp.zeros((page_rows, page_length, cache_width), jnp.bfloat16)
        .at[local_pages]
        .set(cache_columns.reshape(page_rows, page_length, cache_width))
    )
    heads = queries.shape[1] // HD
    group = tp_index * heads // (HQ // HK)
    key_head = lax.dynamic_slice_in_dim(keyval, group * HD, HD, 1)
    value_head = lax.dynamic_slice_in_dim(keyval, (HK + group) * HD, HD, 1)
    query_heads = queries.reshape(count, heads, HD)
    query_index = seq_index * count + jnp.arange(count, dtype=jnp.int32)
    width = 2 * HD
    code_rows = 2 * count // width
    code = jnp.stack([segment_ids // 256, segment_ids % 256]).astype(jnp.bfloat16).reshape(code_rows, width)
    code = jnp.concatenate([code, jnp.zeros((16 - code_rows % 16, width), jnp.bfloat16)], axis=0)
    own_piece = jnp.concatenate([jnp.concatenate([key_head, value_head], axis=1), code], axis=0)
    reach_steps = lax.axis_size("seq") // 4
    seq_count = lax.axis_size("seq")
    rounds = reach_steps // 2
    core = tp_index % 2
    fetched = []
    for number in range(1, rounds + 1):
        pairs = []
        for source_seq in range(seq_count):
            for lane in range(tp_count):
                target_seq = source_seq + number + rounds * (lane % 2)
                if target_seq < seq_count:
                    pairs.append((source_seq * tp_count + lane, target_seq * tp_count + lane))
        fetched.append(lax.ppermute(own_piece, ("seq", "tp"), pairs))
    swapped = lax.ppermute(jnp.stack(fetched), "tp", [(lane, lane ^ 1) for lane in range(tp_count)])
    pieces = [(own_piece, 0)]
    pieces += [(piece, number + 1 + rounds * core) for number, piece in enumerate(fetched)]
    pieces += [(swapped[number], number + 1 + rounds * (1 - core)) for number in range(rounds)]

    def visit(carry, piece, number):
        start = (seq_index - number) * count
        key_index = start + jnp.arange(count, dtype=jnp.int32)
        coded = piece[count : count + code_rows].reshape(2, count).astype(jnp.int32)
        segment_piece = coded[0] * 256 + coded[1]
        allowed = (
            (segment_piece[None, :] == segment_ids[:, None])
            & (key_index[None, :] <= query_index[:, None])
            & (key_index[None, :] >= 0)
        )
        return attend_block(carry, query_heads, piece[:count, :HD], piece[:count, HD:], allowed)

    state = (
        jnp.full((count, heads), NEGATIVE, jnp.float32),
        jnp.zeros((count, heads), jnp.float32),
        jnp.zeros((count, heads, HD), jnp.float32),
    )
    for piece, number in pieces:
        state = visit(state, piece, number)
    attended = (state[2] / state[1][:, :, None]).astype(jnp.bfloat16).reshape(count, heads * HD)
    hidden_part = w_gate.shape[2]
    packed = jnp.concatenate([w_gate[0], w_up[0], w_down[0].T], axis=1)
    partner_pairs = [(source, source ^ 2) for source in range(tp_count)]
    across_front = lax.ppermute(packed[:, : 2 * hidden_part], "tp", partner_pairs)
    attended, across_front = lax.optimization_barrier((attended, across_front))
    across = jnp.concatenate(
        [across_front, lax.ppermute(packed[:, 2 * hidden_part :], "tp", partner_pairs)], axis=1
    )
    sibling = [(source, source ^ 1) for source in range(tp_count)]
    weight_parts = [packed, across, lax.ppermute(packed, "tp", sibling), lax.ppermute(across, "tp", sibling)]
    projected = jnp.dot(attended, w_out, preferred_element_type=jnp.float32)
    experts = lax.axis_size("seq") * w_gate.shape[0]
    choose = expert_picks.shape[1]
    capacity = count * choose * 5 // (4 * experts)
    share = capacity // tp_count
    slots = experts * share
    onehot = (expert_picks[:, :, None] == jnp.arange(experts, dtype=jnp.int32)[None, None, :]).astype(
        jnp.float32
    )
    earlier = (
        jnp.arange(count, dtype=jnp.int32)[:, None] > jnp.arange(count, dtype=jnp.int32)[None, :]
    ).astype(jnp.bfloat16)
    before = jnp.dot(
        earlier, jnp.sum(onehot, axis=1).astype(jnp.bfloat16), preferred_element_type=jnp.float32
    )
    ranks = jnp.sum(before[:, None, :] * onehot, axis=2).astype(jnp.int32)
    owner = ranks // share
    slot = expert_picks * share + ranks % share
    mine_slot = jnp.where(owner == tp_index, slot, slots)
    slot_range = jnp.arange(slots, dtype=jnp.int32)
    placing = jnp.sum(
        (mine_slot[:, :, None] == slot_range[None, None, :]).astype(jnp.bfloat16), axis=1
    ).T
    part_width = tokens.shape[1] // tp_count
    sibling_sum = lax.ppermute(projected.astype(jnp.bfloat16), "tp", sibling)
    chip_sum = projected + sibling_sum.astype(jnp.float32)
    half_width = chip_sum.shape[1] // 2
    own_half = lax.dynamic_slice_in_dim(chip_sum, core * half_width, half_width, 1)
    partner = [(lane, lane ^ 2) for lane in range(tp_count)]
    own_half = own_half + lax.ppermute(own_half.astype(jnp.bfloat16), "tp", partner).astype(jnp.float32)
    other_half = lax.ppermute(own_half.astype(jnp.bfloat16), "tp", sibling).astype(jnp.float32)
    first = core == 0
    summed = jnp.concatenate(
        [jnp.where(first, own_half, other_half), jnp.where(first, other_half, own_half)], axis=1
    )
    summed, weight_parts = lax.optimization_barrier((summed, weight_parts))
    residual = tokens.astype(jnp.float32) + summed
    mixed_in = row_norm(residual, ffn_gain).astype(jnp.bfloat16)
    columns = mixed_in.shape[1]
    rows = jnp.dot(placing, mixed_in, preferred_element_type=jnp.float32).astype(jnp.bfloat16)
    arrived = lax.all_to_all(rows, "seq", split_axis=0, concat_axis=0, tiled=True)
    gate_full = jnp.concatenate([part[:, :hidden_part] for part in weight_parts], axis=1)
    up_full = jnp.concatenate([part[:, hidden_part : 2 * hidden_part] for part in weight_parts], axis=1)
    down_full = jnp.concatenate([part[:, 2 * hidden_part :] for part in weight_parts], axis=1).T
    gate_part = jnp.dot(arrived, gate_full, preferred_element_type=jnp.float32)
    up_part = jnp.dot(arrived, up_full, preferred_element_type=jnp.float32)
    hidden = (jax.nn.relu(gate_part) * up_part).astype(jnp.bfloat16)
    expert_out = jnp.dot(hidden, down_full, preferred_element_type=jnp.float32).astype(jnp.bfloat16)
    sources = lax.axis_size("seq")
    outgoing = (
        expert_out.reshape(sources, share, tp_count, part_width)
        .transpose(0, 2, 1, 3)
        .reshape(sources * tp_count * share, part_width)
    )
    mine = lax.all_to_all(outgoing, ("seq", "tp"), split_axis=0, concat_axis=0, tiled=True)
    residual_part = lax.dynamic_slice_in_dim(residual, tp_index * part_width, part_width, 1)
    every_slot = jnp.arange(experts * capacity, dtype=jnp.int32)
    picked = (expert_picks * capacity + ranks)[:, :, None] == every_slot[None, None, :]
    scales = jnp.sum(jnp.where(picked, gate_weights[:, :, None], 0.0), axis=1)
    high = scales.astype(jnp.bfloat16)
    low = (scales - high.astype(jnp.float32)).astype(jnp.bfloat16)
    both = jnp.dot(jnp.concatenate([high, low], axis=0), mine, preferred_element_type=jnp.float32)
    mixture = both[:count] + both[count:]
    layer_out = (residual_part + mixture).astype(jnp.bfloat16)
    return (layer_out, kv_pages)


def solution(mesh):
    placed = (
        P("seq", None),
        P("seq"),
        P(),
        P(None, "tp"),
        P(),
        P("tp", None),
        P(),
        P("seq", None, "tp"),
        P("seq", None, "tp"),
        P("seq", "tp", None),
        P("seq", None),
        P("seq", None),
        P("seq"),
    )
    return jax.shard_map(
        per_device,
        mesh=mesh,
        in_specs=placed,
        out_specs=(P("seq", "tp"), P("seq", None, "tp")),
        check_vma=False,
    )
```

```python
import jax
import jax.numpy as jnp
from jax import lax
from jax.sharding import PartitionSpec as P

HQ = 12
HK = 2
HD = 128


EPSILON = 1e-06
NEGATIVE = -1e30


def shifted(value, axis, steps):
    count = lax.axis_size(axis)
    leading, last = (max(0, -steps), min(count, count - steps))
    return lax.ppermute(value, axis, [(source, source + steps) for source in range(leading, last)])


def row_norm(values, gain):
    values = values.astype(jnp.float32)
    factor = lax.rsqrt(jnp.mean(values * values, axis=-1, keepdims=True) + EPSILON)
    return values * factor * gain


def attend_block(carry, queries, key_block, value_block, allowed):
    running, total, accum = carry
    scores = jnp.einsum(
        "qhd,kd->qhk", queries, key_block, preferred_element_type=jnp.float32
    ) * HD ** (-0.5)
    open_mask = allowed[:, None, :]
    highest = jnp.max(jnp.where(open_mask, scores, NEGATIVE), axis=2)
    renewed = jnp.maximum(running, highest)
    weights = jnp.where(open_mask, jnp.exp(scores - renewed[:, :, None]), 0.0)
    factor = jnp.exp(running - renewed)
    total = total * factor + jnp.sum(weights, axis=2)
    accum = accum * factor[:, :, None] + jnp.einsum(
        "qhk,kd->qhd", weights.astype(jnp.bfloat16), value_block, preferred_element_type=jnp.float32
    )
    return (renewed, total, accum)


def per_device(
    tokens,
    segment_ids,
    attn_gain,
    w_query,
    w_kv,
    w_out,
    ffn_gain,
    w_gate,
    w_up,
    w_down,
    expert_picks,
    gate_weights,
    page_table,
):
    count = tokens.shape[0]
    seq_index = lax.axis_index("seq")
    tp_index = lax.axis_index("tp")
    tp_count = lax.axis_size("tp")
    normed = row_norm(tokens, attn_gain).astype(jnp.bfloat16)
    queries = jnp.dot(normed, w_query, preferred_element_type=jnp.float32).astype(jnp.bfloat16)
    keyval = jnp.dot(normed, w_kv, preferred_element_type=jnp.float32).astype(jnp.bfloat16)
    cache_width = keyval.shape[1] // tp_count
    cache_columns = lax.dynamic_slice_in_dim(keyval, tp_index * cache_width, cache_width, 1)
    page_rows = page_table.shape[0]
    page_length = count // page_rows
    local_pages = page_table - seq_index * page_rows
    kv_pages = (
        jnp.zeros((page_rows, page_length, cache_width), jnp.bfloat16)
        .at[local_pages]
        .set(cache_columns.reshape(page_rows, page_length, cache_width))
    )
    heads = queries.shape[1] // HD
    group = tp_index * heads // (HQ // HK)
    key_head = lax.dynamic_slice_in_dim(keyval, group * HD, HD, 1)
    value_head = lax.dynamic_slice_in_dim(keyval, (HK + group) * HD, HD, 1)
    query_heads = queries.reshape(count, heads, HD)
    query_index = seq_index * count + jnp.arange(count, dtype=jnp.int32)
    width = 2 * HD
    code_rows = 2 * count // width
    code = jnp.stack([segment_ids // 256, segment_ids % 256]).astype(jnp.bfloat16).reshape(code_rows, width)
    code = jnp.concatenate([code, jnp.zeros((16 - code_rows % 16, width), jnp.bfloat16)], axis=0)
    own_piece = jnp.concatenate([jnp.concatenate([key_head, value_head], axis=1), code], axis=0)
    reach_steps = lax.axis_size("seq") // 4
    seq_count = lax.axis_size("seq")
    rounds = reach_steps // 2
    core = tp_index % 2
    fetched = []
    for number in range(1, rounds + 1):
        pairs = []
        for source_seq in range(seq_count):
            for lane in range(tp_count):
                target_seq = source_seq + number + rounds * (lane % 2)
                if target_seq < seq_count:
                    pairs.append((source_seq * tp_count + lane, target_seq * tp_count + lane))
        fetched.append(lax.ppermute(own_piece, ("seq", "tp"), pairs))
    swapped = lax.ppermute(jnp.stack(fetched), "tp", [(lane, lane ^ 1) for lane in range(tp_count)])
    pieces = [(own_piece, 0)]
    pieces += [(piece, number + 1 + rounds * core) for number, piece in enumerate(fetched)]
    pieces += [(swapped[number], number + 1 + rounds * (1 - core)) for number in range(rounds)]

    def visit(carry, piece, number):
        start = (seq_index - number) * count
        key_index = start + jnp.arange(count, dtype=jnp.int32)
        coded = piece[count : count + code_rows].reshape(2, count).astype(jnp.int32)
        segment_piece = coded[0] * 256 + coded[1]
        allowed = (
            (segment_piece[None, :] == segment_ids[:, None])
            & (key_index[None, :] <= query_index[:, None])
            & (key_index[None, :] >= 0)
        )
        return attend_block(carry, query_heads, piece[:count, :HD], piece[:count, HD:], allowed)

    state = (
        jnp.full((count, heads), NEGATIVE, jnp.float32),
        jnp.zeros((count, heads), jnp.float32),
        jnp.zeros((count, heads, HD), jnp.float32),
    )
    for piece, number in pieces:
        state = visit(state, piece, number)
    attended = (state[2] / state[1][:, :, None]).astype(jnp.bfloat16).reshape(count, heads * HD)
    hidden_part = w_gate.shape[2]
    packed = jnp.concatenate([w_gate[0], w_up[0], w_down[0].T], axis=1)
    across = lax.ppermute(packed, "tp", [(source, source ^ 2) for source in range(tp_count)])
    attended, across = lax.optimization_barrier((attended, across))
    sibling = [(source, source ^ 1) for source in range(tp_count)]
    weight_parts = [packed, across, lax.ppermute(packed, "tp", sibling), lax.ppermute(across, "tp", sibling)]
    projected = jnp.dot(attended, w_out, preferred_element_type=jnp.float32)
    experts = lax.axis_size("seq") * w_gate.shape[0]
    choose = expert_picks.shape[1]
    capacity = count * choose * 5 // (4 * experts)
    share = capacity // tp_count
    slots = experts * share
    onehot = (expert_picks[:, :, None] == jnp.arange(experts, dtype=jnp.int32)[None, None, :]).astype(
        jnp.float32
    )
    earlier = (
        jnp.arange(count, dtype=jnp.int32)[:, None] > jnp.arange(count, dtype=jnp.int32)[None, :]
    ).astype(jnp.bfloat16)
    before = jnp.dot(
        earlier, jnp.sum(onehot, axis=1).astype(jnp.bfloat16), preferred_element_type=jnp.float32
    )
    ranks = jnp.sum(before[:, None, :] * onehot, axis=2).astype(jnp.int32)
    owner = ranks // share
    slot = expert_picks * share + ranks % share
    mine_slot = jnp.where(owner == tp_index, slot, slots)
    slot_range = jnp.arange(slots, dtype=jnp.int32)
    placing = jnp.sum(
        (mine_slot[:, :, None] == slot_range[None, None, :]).astype(jnp.bfloat16), axis=1
    ).T
    part_width = tokens.shape[1] // tp_count
    sibling_sum = lax.ppermute(projected.astype(jnp.bfloat16), "tp", sibling)
    chip_sum = projected + sibling_sum.astype(jnp.float32)
    half_width = chip_sum.shape[1] // 2
    own_half = lax.dynamic_slice_in_dim(chip_sum, core * half_width, half_width, 1)
    partner = [(lane, lane ^ 2) for lane in range(tp_count)]
    own_half = own_half + lax.ppermute(own_half.astype(jnp.bfloat16), "tp", partner).astype(jnp.float32)
    other_half = lax.ppermute(own_half.astype(jnp.bfloat16), "tp", sibling).astype(jnp.float32)
    first = core == 0
    summed = jnp.concatenate(
        [jnp.where(first, own_half, other_half), jnp.where(first, other_half, own_half)], axis=1
    )
    summed, weight_parts = lax.optimization_barrier((summed, weight_parts))
    residual = tokens.astype(jnp.float32) + summed
    mixed_in = row_norm(residual, ffn_gain).astype(jnp.bfloat16)
    columns = mixed_in.shape[1]
    rows = jnp.dot(placing, mixed_in, preferred_element_type=jnp.float32).astype(jnp.bfloat16)
    arrived = lax.all_to_all(rows, "seq", split_axis=0, concat_axis=0, tiled=True)
    gate_up = jnp.concatenate(
        [part[:, :hidden_part] for part in weight_parts]
        + [part[:, hidden_part : 2 * hidden_part] for part in weight_parts],
        axis=1,
    )
    down_full = jnp.concatenate([part[:, 2 * hidden_part :] for part in weight_parts], axis=1).T
    arrived, gate_up, down_full = lax.optimization_barrier((arrived, gate_up, down_full))
    both_parts = jnp.dot(arrived, gate_up, preferred_element_type=jnp.float32)
    gate_part = both_parts[:, : tp_count * hidden_part]
    up_part = both_parts[:, tp_count * hidden_part :]
    hidden = (jax.nn.relu(gate_part) * up_part).astype(jnp.bfloat16)
    expert_out = jnp.dot(hidden, down_full, preferred_element_type=jnp.float32).astype(jnp.bfloat16)
    sources = lax.axis_size("seq")
    outgoing = (
        expert_out.reshape(sources, share, tp_count, part_width)
        .transpose(0, 2, 1, 3)
        .reshape(sources * tp_count * share, part_width)
    )
    mine = lax.all_to_all(outgoing, ("seq", "tp"), split_axis=0, concat_axis=0, tiled=True)
    residual_part = lax.dynamic_slice_in_dim(residual, tp_index * part_width, part_width, 1)
    every_slot = jnp.arange(experts * capacity, dtype=jnp.int32)
    picked = (expert_picks * capacity + ranks)[:, :, None] == every_slot[None, None, :]
    scales = jnp.sum(jnp.where(picked, gate_weights[:, :, None], 0.0), axis=1)
    high = scales.astype(jnp.bfloat16)
    low = (scales - high.astype(jnp.float32)).astype(jnp.bfloat16)
    both = jnp.dot(jnp.concatenate([high, low], axis=0), mine, preferred_element_type=jnp.float32)
    mixture = both[:count] + both[count:]
    layer_out = (residual_part + mixture).astype(jnp.bfloat16)
    return (layer_out, kv_pages)


def solution(mesh):
    placed = (
        P("seq", None),
        P("seq"),
        P(),
        P(None, "tp"),
        P(),
        P("tp", None),
        P(),
        P("seq", None, "tp"),
        P("seq", None, "tp"),
        P("seq", "tp", None),
        P("seq", None),
        P("seq", None),
        P("seq"),
    )
    return jax.shard_map(
        per_device,
        mesh=mesh,
        in_specs=placed,
        out_specs=(P("seq", "tp"), P("seq", None, "tp")),
        check_vma=False,
    )
```

```python
import jax
import jax.numpy as jnp
from jax import lax
from jax.sharding import PartitionSpec as P

HQ = 12
HK = 2
HD = 128


EPSILON = 1e-06
NEGATIVE = -1e30


def row_norm(values, gain):
    values = values.astype(jnp.float32)
    factor = lax.rsqrt(jnp.mean(values * values, axis=-1, keepdims=True) + EPSILON)
    return values * factor * gain


def attend_block(carry, queries, key_block, value_block, allowed):
    running, total, accum = carry
    scores = jnp.einsum(
        "qhd,kd->qhk", queries, key_block, preferred_element_type=jnp.float32
    ) * HD ** (-0.5)
    open_mask = allowed[:, None, :]
    highest = jnp.max(jnp.where(open_mask, scores, NEGATIVE), axis=2)
    renewed = jnp.maximum(running, highest)
    weights = jnp.where(open_mask, jnp.exp(scores - renewed[:, :, None]), 0.0)
    factor = jnp.exp(running - renewed)
    total = total * factor + jnp.sum(weights, axis=2)
    accum = accum * factor[:, :, None] + jnp.einsum(
        "qhk,kd->qhd", weights.astype(jnp.bfloat16), value_block, preferred_element_type=jnp.float32
    )
    return (renewed, total, accum)


def per_device(
    tokens,
    segment_ids,
    attn_gain,
    w_query,
    w_kv,
    w_out,
    ffn_gain,
    w_gate,
    w_up,
    w_down,
    expert_picks,
    gate_weights,
    page_table,
):
    count = tokens.shape[0]
    seq_index = lax.axis_index("seq")
    tp_index = lax.axis_index("tp")
    tp_count = lax.axis_size("tp")
    normed = row_norm(tokens, attn_gain).astype(jnp.bfloat16)
    queries = jnp.dot(normed, w_query, preferred_element_type=jnp.float32).astype(jnp.bfloat16)
    keyval = jnp.dot(normed, w_kv, preferred_element_type=jnp.float32).astype(jnp.bfloat16)
    cache_width = keyval.shape[1] // tp_count
    cache_columns = lax.dynamic_slice_in_dim(keyval, tp_index * cache_width, cache_width, 1)
    page_rows = page_table.shape[0]
    page_length = count // page_rows
    local_pages = page_table - seq_index * page_rows
    kv_pages = (
        jnp.zeros((page_rows, page_length, cache_width), jnp.bfloat16)
        .at[local_pages]
        .set(cache_columns.reshape(page_rows, page_length, cache_width))
    )
    heads = queries.shape[1] // HD
    group = tp_index * heads // (HQ // HK)
    key_head = lax.dynamic_slice_in_dim(keyval, group * HD, HD, 1)
    value_head = lax.dynamic_slice_in_dim(keyval, (HK + group) * HD, HD, 1)
    query_heads = queries.reshape(count, heads, HD)
    query_index = seq_index * count + jnp.arange(count, dtype=jnp.int32)
    width = 2 * HD
    code_rows = 2 * count // width
    code = jnp.stack([segment_ids // 256, segment_ids % 256]).astype(jnp.bfloat16).reshape(code_rows, width)
    code = jnp.concatenate([code, jnp.zeros((16 - code_rows % 16, width), jnp.bfloat16)], axis=0)
    own_piece = jnp.concatenate([jnp.concatenate([key_head, value_head], axis=1), code], axis=0)
    reach_steps = lax.axis_size("seq") // 4
    seq_count = lax.axis_size("seq")
    rounds = reach_steps // 2
    core = tp_index % 2
    fetched = []
    for number in range(1, rounds + 1):
        pairs = []
        for source_seq in range(seq_count):
            for lane in range(tp_count):
                target_seq = source_seq + number + rounds * (lane % 2)
                if target_seq < seq_count:
                    pairs.append((source_seq * tp_count + lane, target_seq * tp_count + lane))
        fetched.append(lax.ppermute(own_piece, ("seq", "tp"), pairs))
    swapped = lax.ppermute(jnp.stack(fetched), "tp", [(lane, lane ^ 1) for lane in range(tp_count)])
    pieces = [(own_piece, 0)]
    pieces += [(piece, number + 1 + rounds * core) for number, piece in enumerate(fetched)]
    pieces += [(swapped[number], number + 1 + rounds * (1 - core)) for number in range(rounds)]

    def visit(carry, piece, number):
        start = (seq_index - number) * count
        key_index = start + jnp.arange(count, dtype=jnp.int32)
        coded = piece[count : count + code_rows].reshape(2, count).astype(jnp.int32)
        segment_piece = coded[0] * 256 + coded[1]
        allowed = (
            (segment_piece[None, :] == segment_ids[:, None])
            & (key_index[None, :] <= query_index[:, None])
            & (key_index[None, :] >= 0)
        )
        return attend_block(carry, query_heads, piece[:count, :HD], piece[:count, HD:], allowed)

    state = (
        jnp.full((count, heads), NEGATIVE, jnp.float32),
        jnp.zeros((count, heads), jnp.float32),
        jnp.zeros((count, heads, HD), jnp.float32),
    )
    for piece, number in pieces:
        state = visit(state, piece, number)
    attended = (state[2] / state[1][:, :, None]).astype(jnp.bfloat16).reshape(count, heads * HD)
    hidden_part = w_gate.shape[2]
    packed = jnp.concatenate([w_gate[0], w_up[0], w_down[0].T], axis=1)
    across = lax.ppermute(packed, "tp", [(source, source ^ 2) for source in range(tp_count)])
    attended, across = lax.optimization_barrier((attended, across))
    sibling = [(source, source ^ 1) for source in range(tp_count)]
    weight_parts = [packed, across, lax.ppermute(packed, "tp", sibling), lax.ppermute(across, "tp", sibling)]
    projected = jnp.dot(attended, w_out, preferred_element_type=jnp.float32)
    experts = lax.axis_size("seq") * w_gate.shape[0]
    choose = expert_picks.shape[1]
    capacity = count * choose * 5 // (4 * experts)
    share = capacity // tp_count
    slots = experts * share
    onehot = (expert_picks[:, :, None] == jnp.arange(experts, dtype=jnp.int32)[None, None, :]).astype(
        jnp.float32
    )
    earlier = (
        jnp.arange(count, dtype=jnp.int32)[:, None] > jnp.arange(count, dtype=jnp.int32)[None, :]
    ).astype(jnp.bfloat16)
    before = jnp.dot(
        earlier, jnp.sum(onehot, axis=1).astype(jnp.bfloat16), preferred_element_type=jnp.float32
    )
    ranks = jnp.sum(before[:, None, :] * onehot, axis=2).astype(jnp.int32)
    owner = ranks // share
    slot = expert_picks * share + ranks % share
    mine_slot = jnp.where(owner == tp_index, slot, slots)
    slot_range = jnp.arange(slots, dtype=jnp.int32)
    placing = jnp.sum(
        (mine_slot[:, :, None] == slot_range[None, None, :]).astype(jnp.bfloat16), axis=1
    ).T
    part_width = tokens.shape[1] // tp_count
    sibling_sum = lax.ppermute(projected.astype(jnp.bfloat16), "tp", sibling)
    chip_sum = projected + sibling_sum.astype(jnp.float32)
    half_width = chip_sum.shape[1] // 2
    own_half = lax.dynamic_slice_in_dim(chip_sum, core * half_width, half_width, 1)
    partner = [(lane, lane ^ 2) for lane in range(tp_count)]
    own_half = own_half + lax.ppermute(own_half.astype(jnp.bfloat16), "tp", partner).astype(jnp.float32)
    other_half = lax.ppermute(own_half.astype(jnp.bfloat16), "tp", sibling).astype(jnp.float32)
    first = core == 0
    summed = jnp.concatenate(
        [jnp.where(first, own_half, other_half), jnp.where(first, other_half, own_half)], axis=1
    )
    summed, weight_parts = lax.optimization_barrier((summed, weight_parts))
    residual = tokens.astype(jnp.float32) + summed
    mixed_in = row_norm(residual, ffn_gain).astype(jnp.bfloat16)
    rows = jnp.dot(placing, mixed_in, preferred_element_type=jnp.float32).astype(jnp.bfloat16)
    arrived = lax.all_to_all(rows, "seq", split_axis=0, concat_axis=0, tiled=True)
    gate_up = jnp.concatenate(
        [part[:, :hidden_part] for part in weight_parts]
        + [part[:, hidden_part : 2 * hidden_part] for part in weight_parts],
        axis=1,
    )
    down_full = jnp.concatenate([part[:, 2 * hidden_part :] for part in weight_parts], axis=1).T
    arrived, gate_up, down_full = lax.optimization_barrier((arrived, gate_up, down_full))
    both_parts = jnp.dot(arrived, gate_up, preferred_element_type=jnp.float32)
    gate_part = both_parts[:, : tp_count * hidden_part]
    up_part = both_parts[:, tp_count * hidden_part :]
    hidden = (jax.nn.relu(gate_part) * up_part).astype(jnp.bfloat16)
    expert_out = jnp.dot(hidden, down_full, preferred_element_type=jnp.float32).astype(jnp.bfloat16)
    sources = lax.axis_size("seq")
    outgoing = (
        expert_out.reshape(sources, share, tp_count, part_width)
        .transpose(0, 2, 1, 3)
        .reshape(sources * tp_count * share, part_width)
    )
    mine = lax.all_to_all(outgoing, ("seq", "tp"), split_axis=0, concat_axis=0, tiled=True)
    residual_part = lax.dynamic_slice_in_dim(residual, tp_index * part_width, part_width, 1)
    every_slot = jnp.arange(experts * capacity, dtype=jnp.int32)
    picked = (expert_picks * capacity + ranks)[:, :, None] == every_slot[None, None, :]
    scales = jnp.sum(jnp.where(picked, gate_weights[:, :, None], 0.0), axis=1)
    high = scales.astype(jnp.bfloat16)
    low = (scales - high.astype(jnp.float32)).astype(jnp.bfloat16)
    both = jnp.dot(jnp.concatenate([high, low], axis=0), mine, preferred_element_type=jnp.float32)
    mixture = both[:count] + both[count:]
    layer_out = (residual_part + mixture).astype(jnp.bfloat16)
    return (layer_out, kv_pages)


def solution(mesh):
    placed = (
        P("seq", None),
        P("seq"),
        P(),
        P(None, "tp"),
        P(),
        P("tp", None),
        P(),
        P("seq", None, "tp"),
        P("seq", None, "tp"),
        P("seq", "tp", None),
        P("seq", None),
        P("seq", None),
        P("seq"),
    )

    return jax.shard_map(
        per_device,
        mesh=mesh,
        in_specs=placed,
        out_specs=(P("seq", "tp"), P("seq", None, "tp")),
        check_vma=False,
    )
```
